256 devices in a mesh: date: 64 (over x, y, z_lo, core), rng: 4 (over z_hi).
Axes of the slice: x: 4, y: 4, z: 8 (z_hi: 4, z_lo: 2; z = z_hi * 2 + z_lo), core: 2. Of those that a mesh axis runs over, the one named last changes fastest.
Arguments:
- slc_re: bfloat16 [64, 2048, 512], P('date', None, 'rng'), may hold values from -170 to 170
- slc_im: bfloat16 [64, 2048, 512], P('date', None, 'rng'), may hold values from -170 to 170
- ref_date: int32 [1], replicated, may hold values from 0 to 63
- gain: float32 [2048], replicated, may hold values from 0.25 to 2
- bperp: int32 [64], replicated, may hold values from -200 to 199
- tdays: int32 [64], replicated, may hold values from 0 to 1899
- mask: int32 [2048, 512], P(None, 'rng'), may hold values from 0 to 1, as said below
Outputs:
- periodogram: float32 [2048, 512, 256], P('date', 'rng')
The draws below stay inside these ranges and needn't reach their ends.
Inputs may be any that keep to these rules, and one draw needn't show every extreme that they name: `mask`: each aligned block of 32 lines by 128 range columns holds exactly 1024 candidates.
All inputs are finite; a program needn't handle non-finite values.
Results may differ from the reference program's by a relative error of at most 0.0067.
Values may be sent and summed in bfloat16 or wider, within the bound.
No kernel may reach another device: no remote copies, remote signals or barrier semaphores. Data moves between devices by JAX's collectives and lax.ppermute only.
A program may use at most 64 MiB of HBM per device.

```python
import math
import jax
import jax.numpy as jnp
from jax import lax

LINES = 2048
RG_DEV = 128
HGRID = 16
VGRID = 16
PHASE_Q = 1024
DATES = 64
RG = 512
LINES_DEV = 32
PS_DEV = 1024


def slc_levels(key):
    date_draw = jax.random.uniform(jax.random.fold_in(key, 3), (DATES, 1, 1), jnp.float32, 0.0, 1.0)
    date_levels = jnp.exp(date_draw * math.log(10.0))
    columns = jnp.arange(RG).astype(jnp.float32) / (RG - 1)
    column_slope = jnp.exp(columns * math.log(3.0))
    rough_draw = jax.random.uniform(jax.random.fold_in(key, 4), (1, 1, RG), jnp.float32, -1.0, 1.0)
    column_rough = jnp.exp(rough_draw * math.log(2.0))
    return date_levels * column_slope[None, None, :] * column_rough


def slc_part(key, fold_value):
    levels = slc_levels(key)
    samples = jax.random.truncated_normal(jax.random.fold_in(key, fold_value), -4.0, 4.0, (DATES, LINES, RG), jnp.float32) * 0.7071
    return (samples * levels).astype(jnp.bfloat16)


def draw_slc_re(key, part):
    return slc_part(key, 1)


def draw_slc_im(key, part):
    return slc_part(key, 2)


def draw_mask(key, part):
    lines_blocks = LINES // LINES_DEV
    range_blocks = RG // RG_DEV
    block_total = lines_blocks * range_blocks
    block_cells = LINES_DEV * RG_DEV
    key_list = jax.random.split(jax.random.fold_in(key, 11), block_total)
    orders = jax.vmap(lambda block_key: jax.random.permutation(block_key, block_cells))(key_list)
    chosen = (orders < PS_DEV).astype(jnp.int32)
    blocked = chosen.reshape(lines_blocks, range_blocks, LINES_DEV, RG_DEV)
    return jnp.transpose(blocked, (0, 2, 1, 3)).reshape(LINES, RG)


def touch_ends(result, own_key, smallest, high):
    extent = result.shape
    place = [jax.random.randint(jax.random.fold_in(own_key, axis), (), 0, extent[axis]) for axis in range(len(extent))]
    result = result.at[tuple(place)].set(smallest)
    longest = extent.index(max(extent))
    place[longest] = (place[longest] + 1) % extent[longest]
    return result.at[tuple(place)].set(high)


def setup_inputs(seed: int = 0) -> dict:
    arg_keys = jax.random.split(jax.random.key(seed), 8)
    return {
        "slc_re": draw_slc_re(jax.random.fold_in(arg_keys[7], 71), 0),
        "slc_im": draw_slc_im(jax.random.fold_in(arg_keys[7], 71), 0),
        "ref_date": jax.random.randint(arg_keys[2], (1,), 0, DATES).astype(jnp.int32),
        "gain": jnp.clip(jnp.exp(jax.random.uniform(arg_keys[3], (LINES,), jnp.float32, math.log(0.25), math.log(2.0))), 0.25, 2.0),
        "bperp": touch_ends(jax.random.randint(arg_keys[4], (DATES,), -200, 200), jax.random.fold_in(arg_keys[4], 1), -200, 199).astype(jnp.int32),
        "tdays": touch_ends(jax.random.randint(arg_keys[5], (DATES,), 0, 1900), jax.random.fold_in(arg_keys[5], 1), 0, 1899).astype(jnp.int32),
        "mask": draw_mask(jax.random.fold_in(arg_keys[7], 71), 0),
    }


def dft_tables(length):
    positions = jnp.arange(length, dtype=jnp.int32)
    products = positions[:, None] * positions[None, :] % length
    angles = products.astype(jnp.float32) * (2.0 * math.pi / length)
    return (jnp.cos(angles).astype(jnp.bfloat16), jnp.sin(angles).astype(jnp.bfloat16))

def phase_tables(bperp, tdays):
    grid_points = jnp.arange(HGRID * VGRID, dtype=jnp.int32)
    height_step = grid_points // VGRID
    speed_step = grid_points % VGRID
    quanta = (bperp[:, None] * height_step[None, :] + tdays[:, None] * speed_step[None, :]) % PHASE_Q
    angles = quanta.astype(jnp.float32) * (2.0 * math.pi / PHASE_Q)
    phase_re = jnp.cos(angles).astype(jnp.bfloat16)
    phase_im = jnp.sin(angles).astype(jnp.bfloat16)
    upper = jnp.concatenate([phase_re, -phase_im], axis=1)
    lower = jnp.concatenate([phase_im, phase_re], axis=1)
    return jnp.concatenate([upper, lower], axis=0)

def coherence_map(piece_re, piece_im, phase_table):
    date_count = piece_re.shape[0]
    grid_size = phase_table.shape[1] // 2
    wide_re = piece_re.astype(jnp.float32)
    wide_im = piece_im.astype(jnp.float32)
    stacked = jnp.concatenate([wide_re, wide_im], axis=0)
    table_wide = lax.optimization_barrier(phase_table).astype(jnp.float32)
    spectra = jnp.einsum('dp,dg->pg', stacked, table_wide)
    peri_re = spectra[:, :grid_size]
    peri_im = spectra[:, grid_size:]
    pixel_power = lax.optimization_barrier(jnp.sum(wide_re * wide_re + wide_im * wide_im, axis=0)) / date_count
    return (peri_re * peri_re + peri_im * peri_im) / (date_count * jnp.maximum(pixel_power, 1.0))[:, None]

def reference(slc_re, slc_im, ref_date, gain, bperp, tdays, mask):
    wide_re = slc_re.astype(jnp.float32)
    wide_im = slc_im.astype(jnp.float32)
    power = lax.optimization_barrier(jnp.sum(wide_re * wide_re + wide_im * wide_im, axis=(1, 2))) / (LINES * RG)
    scales = lax.rsqrt(power + 1e-06)
    ref_index = ref_date[0].astype(jnp.int32)
    ref_scale = lax.dynamic_index_in_dim(scales, ref_index, 0, keepdims=False)
    ref_re = lax.dynamic_index_in_dim(wide_re, ref_index, 0, keepdims=False) * ref_scale
    ref_im = lax.dynamic_index_in_dim(wide_im, ref_index, 0, keepdims=False) * ref_scale
    cos_table, sin_table = dft_tables(LINES)
    cos_wide = lax.optimization_barrier(cos_table).astype(jnp.float32)
    sin_wide = lax.optimization_barrier(sin_table).astype(jnp.float32)
    weights = gain[:, None]

    def filter_date(inputs):
        date_re, date_im, date_scale = inputs
        own_re = date_re.astype(jnp.float32) * date_scale
        own_im = date_im.astype(jnp.float32) * date_scale
        ifg_re = (own_re * ref_re + own_im * ref_im).astype(jnp.bfloat16)
        ifg_im = (own_im * ref_re - own_re * ref_im).astype(jnp.bfloat16)
        pair = lax.optimization_barrier(jnp.stack([ifg_re, ifg_im])).astype(jnp.float32)
        cos_part = jnp.einsum('fl,klc->kfc', cos_wide, pair)
        sin_part = jnp.einsum('fl,klc->kfc', sin_wide, pair)
        spec_re = cos_part[0] + sin_part[1]
        spec_im = cos_part[1] - sin_part[0]
        held = jnp.stack([(spec_re * weights).astype(jnp.bfloat16), (spec_im * weights).astype(jnp.bfloat16)])
        held = lax.optimization_barrier(held).astype(jnp.float32)
        back_cos = jnp.einsum('fl,kfc->klc', cos_wide, held)
        back_sin = jnp.einsum('fl,kfc->klc', sin_wide, held)
        filt_re = ((back_cos[0] - back_sin[1]) * (1.0 / LINES)).astype(jnp.bfloat16)
        filt_im = ((back_sin[0] + back_cos[1]) * (1.0 / LINES)).astype(jnp.bfloat16)
        return (filt_re, filt_im)
    filt_re, filt_im = lax.map(filter_date, (slc_re, slc_im, scales))
    phase_table = phase_tables(bperp, tdays)
    line_block = 16
    block_count = LINES // line_block
    moved_re = jnp.moveaxis(filt_re.reshape(DATES, block_count, line_block * RG), 1, 0)
    moved_im = jnp.moveaxis(filt_im.reshape(DATES, block_count, line_block * RG), 1, 0)

    def pixel_block(pieces):
        piece_re, piece_im = pieces
        return coherence_map(piece_re, piece_im, phase_table)
    mapped = lax.map(pixel_block, (moved_re, moved_im))
    mapped = mapped.reshape(LINES, RG, HGRID * VGRID)
    return mapped * mask.astype(jnp.float32)[:, :, None]
```

```python
import math

import jax
import jax.numpy as jnp
import numpy as np
from jax import lax
from jax.sharding import PartitionSpec as P

HGRID = 16
VGRID = 16
PHASE_Q = 1024


def dft_table(length):
    split = 64
    hi_count = length // split
    freq = jnp.arange(length, dtype=jnp.int32)[:, None]
    step = 2.0 * math.pi / length
    hi_ang = ((freq * (split * jnp.arange(hi_count, dtype=jnp.int32)[None, :])) % length).astype(
        jnp.float32
    ) * step
    lo_ang = ((freq * jnp.arange(split, dtype=jnp.int32)[None, :]) % length).astype(
        jnp.float32
    ) * step
    hi_c, hi_s = jnp.cos(hi_ang)[:, :, None], jnp.sin(hi_ang)[:, :, None]
    lo_c, lo_s = jnp.cos(lo_ang)[:, None, :], jnp.sin(lo_ang)[:, None, :]
    cos_t = (hi_c * lo_c - hi_s * lo_s).reshape(length, length)
    sin_t = (hi_c * lo_s + hi_s * lo_c).reshape(length, length)
    table = jnp.concatenate([cos_t, sin_t], axis=1).astype(jnp.bfloat16)
    return lax.optimization_barrier(table)


def phase_tables(bperp, tdays):
    grid_points = jnp.arange(HGRID * VGRID, dtype=jnp.int32)
    height_step = grid_points // VGRID
    speed_step = grid_points % VGRID
    quanta = (
        bperp[:, None] * height_step[None, :] + tdays[:, None] * speed_step[None, :]
    ) % PHASE_Q
    angles = quanta.astype(jnp.float32) * (2.0 * math.pi / PHASE_Q)
    phase_re = jnp.cos(angles).astype(jnp.bfloat16)
    phase_im = jnp.sin(angles).astype(jnp.bfloat16)
    upper = jnp.concatenate([phase_re, -phase_im], axis=1)
    lower = jnp.concatenate([phase_im, phase_re], axis=1)
    return jnp.concatenate([upper, lower], axis=0)


def shards(slc_re, slc_im, ref_date, gain, bperp, tdays, mask):
    date_dev, lines, rg_dev = slc_re.shape
    assert date_dev == 1
    n_date = lax.axis_size("date")
    n_rng = lax.axis_size("rng")
    cols = rg_dev // n_date
    lines_dev = lines // n_date
    pixel_total = lines * rg_dev * n_rng
    me = lax.axis_index("date")
    f32 = jnp.float32

    own_re = slc_re[0]
    own_im = slc_im[0]
    wide_re = own_re.astype(f32)
    wide_im = own_im.astype(f32)
    local = jnp.sum(wide_re * wide_re + wide_im * wide_im)
    onehot = jnp.where(jnp.arange(n_date) == me, local, 0.0)
    date_sums = lax.psum(onehot, ("date", "rng"))
    scales = lax.rsqrt(date_sums / pixel_total + 1e-06)

    def to_date_rows(x):
        xt = x.T.reshape(cols, n_date, lines).transpose(1, 0, 2).reshape(n_date * cols, lines)
        return lax.all_to_all(xt, "date", split_axis=0, concat_axis=0, tiled=True)

    x_re = to_date_rows(own_re)
    x_im = to_date_rows(own_im)

    ref_index = ref_date[0]
    ref_scale = scales[ref_index]
    ref_re = lax.dynamic_slice_in_dim(x_re, ref_index * cols, cols, 0).astype(f32) * ref_scale
    ref_im = lax.dynamic_slice_in_dim(x_im, ref_index * cols, cols, 0).astype(f32) * ref_scale
    ref_re = jnp.tile(ref_re, (n_date, 1))
    ref_im = jnp.tile(ref_im, (n_date, 1))
    row_scale = jnp.repeat(scales, cols)[:, None]
    a_re = x_re.astype(f32) * row_scale
    a_im = x_im.astype(f32) * row_scale
    ifg_re = (a_re * ref_re + a_im * ref_im).astype(jnp.bfloat16)
    ifg_im = (a_im * ref_re - a_re * ref_im).astype(jnp.bfloat16)

    table = dft_table(lines)
    rows = n_date * cols
    stacked = jnp.concatenate([ifg_re, ifg_im], axis=0)
    fwd = jnp.dot(stacked, table, preferred_element_type=f32)
    spec_re = fwd[:rows, :lines] + fwd[rows:, lines:]
    spec_im = fwd[rows:, :lines] - fwd[:rows, lines:]
    weights = gain[None, :]
    held = jnp.concatenate(
        [(spec_re * weights).astype(jnp.bfloat16), (spec_im * weights).astype(jnp.bfloat16)],
        axis=0,
    )
    back = jnp.dot(held, table, preferred_element_type=f32)
    filt_re = ((back[:rows, :lines] - back[rows:, lines:]) * (1.0 / lines)).astype(jnp.bfloat16)
    filt_im = ((back[:rows, lines:] + back[rows:, :lines]) * (1.0 / lines)).astype(jnp.bfloat16)

    def to_pixel_rows(x):
        got = lax.all_to_all(x.T, "date", split_axis=0, concat_axis=0, tiled=True)
        return got.reshape(n_date, lines_dev, rows).transpose(1, 0, 2).reshape(-1, rows)

    y_re = to_pixel_rows(filt_re)
    y_im = to_pixel_rows(filt_im)

    grid_size = HGRID * VGRID
    phase = phase_tables(bperp, tdays).reshape(2, n_date, 2, grid_size)
    eye = jnp.eye(cols, dtype=jnp.bfloat16)
    big = (phase[:, :, None, None, :, :] * eye[None, None, :, :, None, None]).reshape(
        2 * rows, cols * 2 * grid_size
    )
    ys = jnp.concatenate([y_re, y_im], axis=1)
    spectra = jnp.dot(ys, big, preferred_element_type=f32).reshape(-1, cols, 2, grid_size)
    peri_re = spectra[:, :, 0, :]
    peri_im = spectra[:, :, 1, :]
    wr = y_re.astype(f32)
    wi = y_im.astype(f32)
    sel = jnp.asarray(np.tile(np.eye(cols, dtype=np.float32), (n_date, 1)))
    pixel_power = (
        jnp.dot(wr * wr + wi * wi, sel, precision=lax.Precision.HIGHEST) / n_date
    )
    result = (peri_re * peri_re + peri_im * peri_im) / (
        n_date * jnp.maximum(pixel_power, 1.0)
    )[:, :, None]
    result = result.reshape(lines_dev, n_date, cols, grid_size).transpose(0, 2, 1, 3)
    result = result.reshape(lines_dev, cols * n_date, grid_size)
    mask_rows = lax.dynamic_slice_in_dim(mask, me * lines_dev, lines_dev, 0)
    return result * mask_rows.astype(f32)[:, :, None]


def solution(mesh):
    in_specs = (P("date", None, "rng"), P("date", None, "rng"), P(), P(), P(), P(), P(None, "rng"))
    out_specs = P("date", "rng", None)
    return jax.shard_map(shards, mesh=mesh, in_specs=in_specs, out_specs=out_specs, check_vma=False)
```

```python
import math

import jax
import jax.numpy as jnp
import numpy as np
from jax import lax
from jax.sharding import PartitionSpec as P

HGRID = 16
VGRID = 16
PHASE_Q = 1024


def dft_table(length):
    split = 64
    hi_count = length // split
    freq = jnp.arange(length, dtype=jnp.int32)[:, None]
    step = 2.0 * math.pi / length
    hi_ang = ((freq * (split * jnp.arange(hi_count, dtype=jnp.int32)[None, :])) % length).astype(
        jnp.float32
    ) * step
    lo_ang = ((freq * jnp.arange(split, dtype=jnp.int32)[None, :]) % length).astype(
        jnp.float32
    ) * step
    hi_c, hi_s = jnp.cos(hi_ang)[:, :, None], jnp.sin(hi_ang)[:, :, None]
    lo_c, lo_s = jnp.cos(lo_ang)[:, None, :], jnp.sin(lo_ang)[:, None, :]
    cos_t = (hi_c * lo_c - hi_s * lo_s).reshape(length, length).astype(jnp.bfloat16)
    sin_t = (hi_c * lo_s + hi_s * lo_c).reshape(length, length).astype(jnp.bfloat16)
    return lax.optimization_barrier((cos_t, sin_t))


def phase_tables(bperp, tdays):
    grid_points = jnp.arange(HGRID * VGRID, dtype=jnp.int32)
    height_step = grid_points // VGRID
    speed_step = grid_points % VGRID
    quanta = (
        bperp[:, None] * height_step[None, :] + tdays[:, None] * speed_step[None, :]
    ) % PHASE_Q
    angles = quanta.astype(jnp.float32) * (2.0 * math.pi / PHASE_Q)
    phase_re = jnp.cos(angles).astype(jnp.bfloat16)
    phase_im = jnp.sin(angles).astype(jnp.bfloat16)
    upper = jnp.concatenate([phase_re, -phase_im], axis=1)
    lower = jnp.concatenate([phase_im, phase_re], axis=1)
    return jnp.concatenate([upper, lower], axis=0)


def shards(slc_re, slc_im, ref_date, gain, bperp, tdays, mask):
    date_dev, lines, rg_dev = slc_re.shape
    assert date_dev == 1
    n_date = lax.axis_size("date")
    n_rng = lax.axis_size("rng")
    cols = rg_dev // n_date
    lines_dev = lines // n_date
    pixel_total = lines * rg_dev * n_rng
    me = lax.axis_index("date")
    f32 = jnp.float32

    own_re = slc_re[0]
    own_im = slc_im[0]
    wide_re = own_re.astype(f32)
    wide_im = own_im.astype(f32)
    local = jnp.sum(wide_re * wide_re + wide_im * wide_im)
    spread = jnp.broadcast_to(local, (n_date * n_rng, 1))
    gathered = lax.all_to_all(spread, ("date", "rng"), split_axis=0, concat_axis=0, tiled=True)
    date_sums = jnp.sum(gathered.reshape(n_date, n_rng), axis=1)
    scales = lax.rsqrt(date_sums / pixel_total + 1e-06)

    both = jnp.stack([own_re.T, own_im.T]).reshape(2, cols, n_date, lines)
    both = both.transpose(2, 0, 1, 3).reshape(n_date * 2 * cols, lines)
    got = lax.all_to_all(both, "date", split_axis=0, concat_axis=0, tiled=True)
    got = got.reshape(n_date, 2, cols, lines)
    x_re = got[:, 0].reshape(n_date * cols, lines)
    x_im = got[:, 1].reshape(n_date * cols, lines)

    ref_index = ref_date[0]
    ref_scale = scales[ref_index]
    ref_re = lax.dynamic_slice_in_dim(x_re, ref_index * cols, cols, 0).astype(f32) * ref_scale
    ref_im = lax.dynamic_slice_in_dim(x_im, ref_index * cols, cols, 0).astype(f32) * ref_scale
    ref_re = jnp.tile(ref_re, (n_date, 1))
    ref_im = jnp.tile(ref_im, (n_date, 1))
    row_scale = jnp.repeat(scales, cols)[:, None]
    a_re = x_re.astype(f32) * row_scale
    a_im = x_im.astype(f32) * row_scale
    ifg_re = (a_re * ref_re + a_im * ref_im).astype(jnp.bfloat16)
    ifg_im = (a_im * ref_re - a_re * ref_im).astype(jnp.bfloat16)

    cos_t, sin_t = dft_table(lines)
    rows = n_date * cols
    stacked = jnp.concatenate([ifg_re, ifg_im], axis=0)
    fc = jnp.dot(stacked, cos_t, preferred_element_type=f32)
    fs = jnp.dot(stacked, sin_t, preferred_element_type=f32)
    spec_re = fc[:rows] + fs[rows:]
    spec_im = fc[rows:] - fs[:rows]
    weights = gain[None, :]
    held = jnp.concatenate(
        [(spec_re * weights).astype(jnp.bfloat16), (spec_im * weights).astype(jnp.bfloat16)],
        axis=0,
    )
    bc = jnp.dot(held, cos_t, preferred_element_type=f32)
    bs = jnp.dot(held, sin_t, preferred_element_type=f32)
    filt_re = ((bc[:rows] - bs[rows:]) * (1.0 / lines)).astype(jnp.bfloat16)
    filt_im = ((bs[:rows] + bc[rows:]) * (1.0 / lines)).astype(jnp.bfloat16)

    pair = jnp.concatenate([filt_re, filt_im], axis=0).T
    got = lax.all_to_all(pair, "date", split_axis=0, concat_axis=0, tiled=True)
    ys = got.reshape(n_date, lines_dev, 2 * rows).transpose(1, 0, 2).reshape(-1, 2 * rows)
    y_re = ys[:, :rows]
    y_im = ys[:, rows:]

    grid_size = HGRID * VGRID
    phase = phase_tables(bperp, tdays).reshape(2, n_date, 2, grid_size)
    eye = jnp.eye(cols, dtype=jnp.bfloat16)
    big = (phase[:, :, None, None, :, :] * eye[None, None, :, :, None, None]).reshape(
        2 * rows, cols * 2 * grid_size
    )
    spectra = jnp.dot(ys, big, preferred_element_type=f32).reshape(-1, cols, 2, grid_size)
    peri_re = spectra[:, :, 0, :]
    peri_im = spectra[:, :, 1, :]
    wr = y_re.astype(f32)
    wi = y_im.astype(f32)
    sel = jnp.asarray(np.tile(np.eye(cols, dtype=np.float32), (n_date, 1)))
    pixel_power = (
        jnp.dot(wr * wr + wi * wi, sel, precision=lax.Precision.HIGHEST) / n_date
    )
    result = (peri_re * peri_re + peri_im * peri_im) / (
        n_date * jnp.maximum(pixel_power, 1.0)
    )[:, :, None]
    result = result.reshape(lines_dev, n_date, cols, grid_size).transpose(0, 2, 1, 3)
    result = result.reshape(lines_dev, cols * n_date, grid_size)
    mask_rows = lax.dynamic_slice_in_dim(mask, me * lines_dev, lines_dev, 0)
    return result * mask_rows.astype(f32)[:, :, None]


def solution(mesh):
    in_specs = (P("date", None, "rng"), P("date", None, "rng"), P(), P(), P(), P(), P(None, "rng"))
    out_specs = P("date", "rng", None)
    return jax.shard_map(shards, mesh=mesh, in_specs=in_specs, out_specs=out_specs, check_vma=False)
```

```python
import math

import jax
import jax.numpy as jnp
from jax import lax
from jax.sharding import PartitionSpec as P

HGRID = 16
VGRID = 16
PHASE_Q = 1024


def dft_table(length):
    split = 64
    hi_count = length // split
    freq = jnp.arange(length, dtype=jnp.int32)[:, None]
    step = 2.0 * math.pi / length
    hi_ang = ((freq * (split * jnp.arange(hi_count, dtype=jnp.int32)[None, :])) % length).astype(
        jnp.float32
    ) * step
    lo_ang = ((freq * jnp.arange(split, dtype=jnp.int32)[None, :]) % length).astype(
        jnp.float32
    ) * step
    hi_c, hi_s = jnp.cos(hi_ang)[:, :, None], jnp.sin(hi_ang)[:, :, None]
    lo_c, lo_s = jnp.cos(lo_ang)[:, None, :], jnp.sin(lo_ang)[:, None, :]
    cos_t = (hi_c * lo_c - hi_s * lo_s).reshape(length, length).astype(jnp.bfloat16)
    sin_t = (hi_c * lo_s + hi_s * lo_c).reshape(length, length).astype(jnp.bfloat16)
    return lax.optimization_barrier((cos_t, sin_t))


def phase_tables(bperp, tdays):
    grid_points = jnp.arange(HGRID * VGRID, dtype=jnp.int32)
    height_step = grid_points // VGRID
    speed_step = grid_points % VGRID
    quanta = (
        bperp[:, None] * height_step[None, :] + tdays[:, None] * speed_step[None, :]
    ) % PHASE_Q
    angles = quanta.astype(jnp.float32) * (2.0 * math.pi / PHASE_Q)
    phase_re = jnp.cos(angles).astype(jnp.bfloat16)
    phase_im = jnp.sin(angles).astype(jnp.bfloat16)
    upper = jnp.concatenate([phase_re, -phase_im], axis=1)
    lower = jnp.concatenate([phase_im, phase_re], axis=1)
    return jnp.concatenate([upper, lower], axis=0)


def shards(slc_re, slc_im, ref_date, gain, bperp, tdays, mask):
    date_dev, lines, rg_dev = slc_re.shape
    assert date_dev == 1
    n_date = lax.axis_size("date")
    n_rng = lax.axis_size("rng")
    cols = rg_dev // n_date
    lines_dev = lines // n_date
    pixel_total = lines * rg_dev * n_rng
    me = lax.axis_index("date")
    f32 = jnp.float32

    own_re = slc_re[0]
    own_im = slc_im[0]
    wide_re = own_re.astype(f32)
    wide_im = own_im.astype(f32)
    local = jnp.sum(wide_re * wide_re + wide_im * wide_im)
    spread = jnp.broadcast_to(local, (n_rng, 1))
    own_sum = jnp.sum(lax.all_to_all(spread, "rng", split_axis=0, concat_axis=0, tiled=True))
    hi = lax.reduce_precision(own_sum, exponent_bits=8, mantissa_bits=7)
    mid = lax.reduce_precision(own_sum - hi, exponent_bits=8, mantissa_bits=7)
    lo = lax.reduce_precision(own_sum - hi - mid, exponent_bits=8, mantissa_bits=7)
    words = jnp.zeros((128,), f32).at[0].set(hi).at[1].set(mid).at[2].set(lo)
    words = jnp.broadcast_to(words.astype(jnp.bfloat16), (n_date, 128))

    both = jnp.stack([own_re.T, own_im.T]).reshape(2, cols, n_date, lines)
    both = both.transpose(2, 0, 1, 3).reshape(n_date, 2 * cols * lines)
    both = jnp.concatenate([both, words], axis=1)
    got = lax.all_to_all(both, "date", split_axis=0, concat_axis=0, tiled=True)
    sums = got[:, 2 * cols * lines:2 * cols * lines + 3].astype(f32)
    date_sums = (sums[:, 0] + sums[:, 1]) + sums[:, 2]
    scales = lax.rsqrt(date_sums / pixel_total + 1e-06)
    got = got[:, :2 * cols * lines].reshape(n_date, 2, cols, lines)
    x_re = got[:, 0].reshape(n_date * cols, lines)
    x_im = got[:, 1].reshape(n_date * cols, lines)

    ref_index = ref_date[0]
    ref_scale = scales[ref_index]
    ref_re = lax.dynamic_slice_in_dim(x_re, ref_index * cols, cols, 0).astype(f32) * ref_scale
    ref_im = lax.dynamic_slice_in_dim(x_im, ref_index * cols, cols, 0).astype(f32) * ref_scale
    ref_re = jnp.tile(ref_re, (n_date, 1))
    ref_im = jnp.tile(ref_im, (n_date, 1))
    row_scale = jnp.repeat(scales, cols)[:, None]
    a_re = x_re.astype(f32) * row_scale
    a_im = x_im.astype(f32) * row_scale
    ifg_re = (a_re * ref_re + a_im * ref_im).astype(jnp.bfloat16)
    ifg_im = (a_im * ref_re - a_re * ref_im).astype(jnp.bfloat16)

    cos_t, sin_t = dft_table(lines)
    rows = n_date * cols
    stacked = jnp.concatenate([ifg_re, ifg_im], axis=0)
    fc = jnp.dot(stacked, cos_t, preferred_element_type=f32)
    fs = jnp.dot(stacked, sin_t, preferred_element_type=f32)
    spec_re = fc[:rows] + fs[rows:]
    spec_im = fc[rows:] - fs[:rows]
    weights = gain[None, :]
    held = jnp.concatenate(
        [(spec_re * weights).astype(jnp.bfloat16), (spec_im * weights).astype(jnp.bfloat16)],
        axis=0,
    )
    bc = jnp.dot(held, cos_t, preferred_element_type=f32)
    bs = jnp.dot(held, sin_t, preferred_element_type=f32)
    filt_re = ((bc[:rows] - bs[rows:]) * (1.0 / lines)).astype(jnp.bfloat16)
    filt_im = ((bs[:rows] + bc[rows:]) * (1.0 / lines)).astype(jnp.bfloat16)

    pair = jnp.concatenate([filt_re, filt_im], axis=0).reshape(2, n_date, cols, lines)
    pair = pair.transpose(2, 0, 1, 3).reshape(2 * rows, lines).T
    got = lax.all_to_all(pair, "date", split_axis=0, concat_axis=0, tiled=True)
    z = got.reshape(n_date, lines_dev, cols, 2 * n_date).transpose(1, 2, 0, 3)
    z = z.reshape(lines_dev * cols * n_date, 2 * n_date)

    grid_size = HGRID * VGRID
    phase = phase_tables(bperp, tdays)
    spectra = jnp.dot(z, phase, preferred_element_type=f32)
    peri_re = spectra[:, :grid_size]
    peri_im = spectra[:, grid_size:]
    wide = z.astype(f32)
    pixel_power = jnp.sum(wide * wide, axis=1) / n_date
    mask_rows = lax.dynamic_slice_in_dim(mask, me * lines_dev, lines_dev, 0)
    mask_px = mask_rows.reshape(-1).astype(f32)
    result = (peri_re * peri_re + peri_im * peri_im) / (
        n_date * jnp.maximum(pixel_power, 1.0)
    )[:, None]
    result = result * mask_px[:, None]
    return result.reshape(lines_dev, cols * n_date, grid_size)


def solution(mesh):
    in_specs = (P("date", None, "rng"), P("date", None, "rng"), P(), P(), P(), P(), P(None, "rng"))
    out_specs = P("date", "rng", None)
    return jax.shard_map(shards, mesh=mesh, in_specs=in_specs, out_specs=out_specs, check_vma=False)
```

```python
import math

import jax
import jax.numpy as jnp
from jax import lax
from jax.sharding import PartitionSpec as P

HGRID = 16
VGRID = 16
PHASE_Q = 1024


def dft_table(length):
    split = 64
    hi_count = length // split
    freq = jnp.arange(length, dtype=jnp.int32)[:, None]
    step = 2.0 * math.pi / length
    hi_ang = ((freq * (split * jnp.arange(hi_count, dtype=jnp.int32)[None, :])) % length).astype(
        jnp.float32
    ) * step
    lo_ang = ((freq * jnp.arange(split, dtype=jnp.int32)[None, :]) % length).astype(
        jnp.float32
    ) * step
    hi_c, hi_s = jnp.cos(hi_ang)[:, :, None], jnp.sin(hi_ang)[:, :, None]
    lo_c, lo_s = jnp.cos(lo_ang)[:, None, :], jnp.sin(lo_ang)[:, None, :]
    cos_t = (hi_c * lo_c - hi_s * lo_s).reshape(length, length).astype(jnp.bfloat16)
    sin_t = (hi_c * lo_s + hi_s * lo_c).reshape(length, length).astype(jnp.bfloat16)
    return lax.optimization_barrier((cos_t, sin_t))


def phase_tables(bperp, tdays):
    grid_points = jnp.arange(HGRID * VGRID, dtype=jnp.int32)
    height_step = grid_points // VGRID
    speed_step = grid_points % VGRID
    quanta = (
        bperp[:, None] * height_step[None, :] + tdays[:, None] * speed_step[None, :]
    ) % PHASE_Q
    angles = quanta.astype(jnp.float32) * (2.0 * math.pi / PHASE_Q)
    phase_re = jnp.cos(angles).astype(jnp.bfloat16)
    phase_im = jnp.sin(angles).astype(jnp.bfloat16)
    upper = jnp.concatenate([phase_re, -phase_im], axis=1)
    lower = jnp.concatenate([phase_im, phase_re], axis=1)
    return jnp.concatenate([upper, lower], axis=0)


def shards(slc_re, slc_im, ref_date, gain, bperp, tdays, mask):
    date_dev, lines, rg_dev = slc_re.shape
    assert date_dev == 1
    n_date = lax.axis_size("date")
    n_rng = lax.axis_size("rng")
    cols = rg_dev // n_date
    lines_dev = lines // n_date
    pixel_total = lines * rg_dev * n_rng
    me = lax.axis_index("date")
    f32 = jnp.float32

    own_re = slc_re[0]
    own_im = slc_im[0]
    wide_re = own_re.astype(f32)
    wide_im = own_im.astype(f32)
    local = jnp.sum(wide_re * wide_re + wide_im * wide_im)
    lane = jnp.arange(lines)
    word = jnp.full((lines,), local)
    hi = lax.reduce_precision(word, exponent_bits=8, mantissa_bits=7)
    mid = lax.reduce_precision(word - hi, exponent_bits=8, mantissa_bits=7)
    lo = lax.reduce_precision(word - hi - mid, exponent_bits=8, mantissa_bits=7)
    word = jnp.where(lane == 0, hi, jnp.where(lane == 1, mid, jnp.where(lane == 2, lo, 0.0)))
    word = jnp.broadcast_to(word.astype(jnp.bfloat16), (n_date, 1, lines))

    both = jnp.stack([own_re.T, own_im.T]).reshape(2, cols, n_date, lines)
    both = both.transpose(2, 0, 1, 3).reshape(n_date, 2 * cols, lines)
    both = jnp.concatenate([both, word], axis=1)
    got = lax.all_to_all(both, "date", split_axis=0, concat_axis=0, tiled=True)
    sums = got[:, 2 * cols, :3].astype(f32)
    part = (sums[:, 0] + sums[:, 1]) + sums[:, 2]
    spread = jnp.broadcast_to(part, (n_rng, n_date))
    date_sums = jnp.sum(
        lax.all_to_all(spread, "rng", split_axis=0, concat_axis=0, tiled=True), axis=0
    )
    scales = lax.rsqrt(date_sums / pixel_total + 1e-06)
    rows = n_date * cols
    x_re = got[:, :cols].reshape(rows, lines).astype(f32)
    x_im = got[:, cols:2 * cols].reshape(rows, lines).astype(f32)

    ref_index = ref_date[0]
    ref_re = jnp.tile(lax.dynamic_slice_in_dim(x_re, ref_index * cols, cols, 0), (n_date, 1))
    ref_im = jnp.tile(lax.dynamic_slice_in_dim(x_im, ref_index * cols, cols, 0), (n_date, 1))
    ifg_re = (x_re * ref_re + x_im * ref_im).astype(jnp.bfloat16)
    ifg_im = (x_im * ref_re - x_re * ref_im).astype(jnp.bfloat16)
    row_scale = (jnp.repeat(scales, cols) * scales[ref_index])[:, None] * (1.0 / lines)

    cos_t, sin_t = dft_table(lines)
    stacked = jnp.concatenate([ifg_re, ifg_im], axis=0)
    fc = jnp.dot(stacked, cos_t, preferred_element_type=f32)
    fs = jnp.dot(stacked, sin_t, preferred_element_type=f32)
    spec_re = fc[:rows] + fs[rows:]
    spec_im = fc[rows:] - fs[:rows]
    weights = gain[None, :]
    held = jnp.concatenate(
        [(spec_re * weights).astype(jnp.bfloat16), (spec_im * weights).astype(jnp.bfloat16)],
        axis=0,
    )
    bc = jnp.dot(held, cos_t, preferred_element_type=f32)
    bs = jnp.dot(held, sin_t, preferred_element_type=f32)
    filt_re = ((bc[:rows] - bs[rows:]) * row_scale).astype(jnp.bfloat16)
    filt_im = ((bs[:rows] + bc[rows:]) * row_scale).astype(jnp.bfloat16)

    pair = jnp.concatenate([filt_re, filt_im], axis=0).reshape(2, n_date, cols, lines)
    pair = pair.transpose(2, 0, 1, 3).reshape(2 * rows, lines).T
    got = lax.all_to_all(pair, "date", split_axis=0, concat_axis=0, tiled=True)
    z = got.reshape(n_date, lines_dev, cols, 2 * n_date).transpose(1, 2, 0, 3)
    z = z.reshape(lines_dev * cols * n_date, 2 * n_date)

    grid_size = HGRID * VGRID
    phase = phase_tables(bperp, tdays)
    spectra = jnp.dot(z, phase, preferred_element_type=f32)
    peri_re = spectra[:, :grid_size]
    peri_im = spectra[:, grid_size:]
    wide = z.astype(f32)
    pixel_power = jnp.sum(wide * wide, axis=1) / n_date
    mask_rows = lax.dynamic_slice_in_dim(mask, me * lines_dev, lines_dev, 0)
    mask_px = mask_rows.reshape(-1).astype(f32)
    result = (peri_re * peri_re + peri_im * peri_im) / (
        n_date * jnp.maximum(pixel_power, 1.0)
    )[:, None]
    result = result * mask_px[:, None]
    return result.reshape(lines_dev, cols * n_date, grid_size)


def solution(mesh):
    in_specs = (P("date", None, "rng"), P("date", None, "rng"), P(), P(), P(), P(), P(None, "rng"))
    out_specs = P("date", "rng", None)
    return jax.shard_map(shards, mesh=mesh, in_specs=in_specs, out_specs=out_specs, check_vma=False)
```

```python
import math

import jax
import jax.numpy as jnp
from jax import lax
from jax.sharding import PartitionSpec as P

HGRID = 16
VGRID = 16
PHASE_Q = 1024


def dft_table(length):
    split = 64
    hi_count = length // split
    freq = jnp.arange(length, dtype=jnp.int32)[:, None]
    step = 2.0 * math.pi / length
    hi_ang = ((freq * (split * jnp.arange(hi_count, dtype=jnp.int32)[None, :])) % length).astype(
        jnp.float32
    ) * step
    lo_ang = ((freq * jnp.arange(split, dtype=jnp.int32)[None, :]) % length).astype(
        jnp.float32
    ) * step
    hi_c, hi_s = jnp.cos(hi_ang)[:, :, None], jnp.sin(hi_ang)[:, :, None]
    lo_c, lo_s = jnp.cos(lo_ang)[:, None, :], jnp.sin(lo_ang)[:, None, :]
    cos_t = (hi_c * lo_c - hi_s * lo_s).reshape(length, length).astype(jnp.bfloat16)
    sin_t = (hi_c * lo_s + hi_s * lo_c).reshape(length, length).astype(jnp.bfloat16)
    return lax.optimization_barrier((cos_t, sin_t))


def phase_tables(bperp, tdays):
    grid_points = jnp.arange(HGRID * VGRID, dtype=jnp.int32)
    height_step = grid_points // VGRID
    speed_step = grid_points % VGRID
    quanta = (
        bperp[:, None] * height_step[None, :] + tdays[:, None] * speed_step[None, :]
    ) % PHASE_Q
    angles = quanta.astype(jnp.float32) * (2.0 * math.pi / PHASE_Q)
    phase_re = jnp.cos(angles).astype(jnp.bfloat16)
    phase_im = jnp.sin(angles).astype(jnp.bfloat16)
    upper = jnp.concatenate([phase_re, -phase_im], axis=1)
    lower = jnp.concatenate([phase_im, phase_re], axis=1)
    return jnp.concatenate([upper, lower], axis=0)


def shards(slc_re, slc_im, ref_date, gain, bperp, tdays, mask):
    date_dev, lines, rg_dev = slc_re.shape
    assert date_dev == 1
    n_date = lax.axis_size("date")
    n_rng = lax.axis_size("rng")
    cols = rg_dev // n_date
    lines_dev = lines // n_date
    pixel_total = lines * rg_dev * n_rng
    me = lax.axis_index("date")
    f32 = jnp.float32

    own_re = slc_re[0]
    own_im = slc_im[0]
    wide_re = own_re.astype(f32)
    wide_im = own_im.astype(f32)
    local = jnp.sum(wide_re * wide_re + wide_im * wide_im)
    own_sum = local
    shift = 1
    while shift < n_rng:
        pairs = [(r, r ^ shift) for r in range(n_rng)]
        own_sum = own_sum + lax.ppermute(own_sum, "rng", pairs)
        shift *= 2
    lane = jnp.arange(128)
    word = jnp.full((128,), own_sum)
    hi = lax.reduce_precision(word, exponent_bits=8, mantissa_bits=7)
    mid = lax.reduce_precision(word - hi, exponent_bits=8, mantissa_bits=7)
    lo = lax.reduce_precision(word - hi - mid, exponent_bits=8, mantissa_bits=7)
    word = jnp.where(lane == 0, hi, jnp.where(lane == 1, mid, jnp.where(lane == 2, lo, 0.0)))
    word = jnp.broadcast_to(word.astype(jnp.bfloat16), (n_date, 2 * cols, 128))

    both = jnp.stack([own_re.T, own_im.T]).reshape(2, cols, n_date, lines)
    both = both.transpose(2, 0, 1, 3).reshape(n_date, 2 * cols, lines)
    both = jnp.concatenate([both, word], axis=2)
    got = lax.all_to_all(both, "date", split_axis=0, concat_axis=0, tiled=True)
    sums = got[:, 0, lines:lines + 3].astype(f32)
    date_sums = (sums[:, 0] + sums[:, 1]) + sums[:, 2]
    scales = lax.rsqrt(date_sums / pixel_total + 1e-06)
    got = got[:, :, :lines].reshape(n_date, 2, cols, lines)
    x_re = got[:, 0].reshape(n_date * cols, lines)
    x_im = got[:, 1].reshape(n_date * cols, lines)

    ref_index = ref_date[0]
    ref_scale = scales[ref_index]
    ref_re = lax.dynamic_slice_in_dim(x_re, ref_index * cols, cols, 0).astype(f32) * ref_scale
    ref_im = lax.dynamic_slice_in_dim(x_im, ref_index * cols, cols, 0).astype(f32) * ref_scale
    ref_re = jnp.tile(ref_re, (n_date, 1))
    ref_im = jnp.tile(ref_im, (n_date, 1))
    row_scale = jnp.repeat(scales, cols)[:, None]
    a_re = x_re.astype(f32) * row_scale
    a_im = x_im.astype(f32) * row_scale
    ifg_re = (a_re * ref_re + a_im * ref_im).astype(jnp.bfloat16)
    ifg_im = (a_im * ref_re - a_re * ref_im).astype(jnp.bfloat16)

    cos_t, sin_t = dft_table(lines)
    rows = n_date * cols
    stacked = jnp.concatenate([ifg_re, ifg_im], axis=0)
    fc = jnp.dot(stacked, cos_t, preferred_element_type=f32)
    fs = jnp.dot(stacked, sin_t, preferred_element_type=f32)
    spec_re = fc[:rows] + fs[rows:]
    spec_im = fc[rows:] - fs[:rows]
    weights = gain[None, :]
    held = jnp.concatenate(
        [(spec_re * weights).astype(jnp.bfloat16), (spec_im * weights).astype(jnp.bfloat16)],
        axis=0,
    )
    bc = jnp.dot(held, cos_t, preferred_element_type=f32)
    bs = jnp.dot(held, sin_t, preferred_element_type=f32)
    filt_re = ((bc[:rows] - bs[rows:]) * (1.0 / lines)).astype(jnp.bfloat16)
    filt_im = ((bs[:rows] + bc[rows:]) * (1.0 / lines)).astype(jnp.bfloat16)

    pair = jnp.concatenate([filt_re, filt_im], axis=0).reshape(2, n_date, cols, lines)
    pair = pair.transpose(2, 0, 1, 3).reshape(2 * rows, lines).T
    got = lax.all_to_all(pair, "date", split_axis=0, concat_axis=0, tiled=True)
    z = got.reshape(n_date, lines_dev, cols, 2 * n_date).transpose(1, 2, 0, 3)
    z = z.reshape(lines_dev * cols * n_date, 2 * n_date)

    grid_size = HGRID * VGRID
    phase = phase_tables(bperp, tdays)
    spectra = jnp.dot(z, phase, preferred_element_type=f32)
    peri_re = spectra[:, :grid_size]
    peri_im = spectra[:, grid_size:]
    wide = z.astype(f32)
    pixel_power = jnp.sum(wide * wide, axis=1) / n_date
    mask_rows = lax.dynamic_slice_in_dim(mask, me * lines_dev, lines_dev, 0)
    mask_px = mask_rows.reshape(-1).astype(f32)
    result = (peri_re * peri_re + peri_im * peri_im) / (
        n_date * jnp.maximum(pixel_power, 1.0)
    )[:, None]
    result = result * mask_px[:, None]
    return result.reshape(lines_dev, cols * n_date, grid_size)


def solution(mesh):
    in_specs = (P("date", None, "rng"), P("date", None, "rng"), P(), P(), P(), P(), P(None, "rng"))
    out_specs = P("date", "rng", None)
    return jax.shard_map(shards, mesh=mesh, in_specs=in_specs, out_specs=out_specs, check_vma=False)
```

```python
import math

import jax
import jax.numpy as jnp
from jax import lax
from jax.sharding import PartitionSpec as P

HGRID = 16
VGRID = 16
PHASE_Q = 1024


def dft_table(length):
    split = 64
    hi_count = length // split
    freq = jnp.arange(length, dtype=jnp.int32)[:, None]
    step = 2.0 * math.pi / length
    hi_ang = ((freq * (split * jnp.arange(hi_count, dtype=jnp.int32)[None, :])) % length).astype(
        jnp.float32
    ) * step
    lo_ang = ((freq * jnp.arange(split, dtype=jnp.int32)[None, :]) % length).astype(
        jnp.float32
    ) * step
    hi_c, hi_s = jnp.cos(hi_ang)[:, :, None], jnp.sin(hi_ang)[:, :, None]
    lo_c, lo_s = jnp.cos(lo_ang)[:, None, :], jnp.sin(lo_ang)[:, None, :]
    cos_t = (hi_c * lo_c - hi_s * lo_s).reshape(length, length).astype(jnp.bfloat16)
    sin_t = (hi_c * lo_s + hi_s * lo_c).reshape(length, length).astype(jnp.bfloat16)
    return lax.optimization_barrier((cos_t, sin_t))


def phase_tables(bperp, tdays):
    grid_points = jnp.arange(HGRID * VGRID, dtype=jnp.int32)
    height_step = grid_points // VGRID
    speed_step = grid_points % VGRID
    quanta = (
        bperp[:, None] * height_step[None, :] + tdays[:, None] * speed_step[None, :]
    ) % PHASE_Q
    angles = quanta.astype(jnp.float32) * (2.0 * math.pi / PHASE_Q)
    phase_re = jnp.cos(angles).astype(jnp.bfloat16)
    phase_im = jnp.sin(angles).astype(jnp.bfloat16)
    upper = jnp.concatenate([phase_re, -phase_im], axis=1)
    lower = jnp.concatenate([phase_im, phase_re], axis=1)
    return jnp.concatenate([upper, lower], axis=0)


def shards(slc_re, slc_im, ref_date, gain, bperp, tdays, mask):
    date_dev, lines, rg_dev = slc_re.shape
    assert date_dev == 1
    n_date = lax.axis_size("date")
    n_rng = lax.axis_size("rng")
    cols = rg_dev // n_date
    lines_dev = lines // n_date
    pixel_total = lines * rg_dev * n_rng
    me = lax.axis_index("date")
    f32 = jnp.float32

    own_re = slc_re[0]
    own_im = slc_im[0]
    wide_re = own_re.astype(f32)
    wide_im = own_im.astype(f32)
    local = jnp.sum(wide_re * wide_re + wide_im * wide_im)
    rng_me = lax.axis_index("rng")
    received = [local] + [
        lax.ppermute(local, "rng", [(r, (r + k) % n_rng) for r in range(n_rng)])
        for k in range(1, n_rng)
    ]
    by_shift = jnp.stack(received)
    by_source = by_shift[(rng_me - jnp.arange(n_rng)) % n_rng]
    own_sum = by_source[0]
    for k in range(1, n_rng):
        own_sum = own_sum + by_source[k]
    lane = jnp.arange(128)
    word = jnp.where(lane < 3, own_sum, 0.0)
    hi = lax.reduce_precision(word, exponent_bits=8, mantissa_bits=7)
    mid = lax.reduce_precision(word - hi, exponent_bits=8, mantissa_bits=7)
    lo = lax.reduce_precision(word - hi - mid, exponent_bits=8, mantissa_bits=7)
    word = jnp.where(lane == 0, hi, jnp.where(lane == 1, mid, lo))
    word = jnp.broadcast_to(word.astype(jnp.bfloat16), (n_date, 2 * cols, 128))

    both = jnp.stack([own_re.T, own_im.T]).reshape(2, cols, n_date, lines)
    both = both.transpose(2, 0, 1, 3).reshape(n_date, 2 * cols, lines)
    both = jnp.concatenate([both, word], axis=2)
    got = lax.all_to_all(both, "date", split_axis=0, concat_axis=0, tiled=True)
    sums = got[:, 0, lines:lines + 3].astype(f32)
    date_sums = (sums[:, 0] + sums[:, 1]) + sums[:, 2]
    scales = lax.rsqrt(date_sums / pixel_total + 1e-06)
    got = got[:, :, :lines].reshape(n_date, 2, cols, lines)
    x_re = got[:, 0].reshape(n_date * cols, lines)
    x_im = got[:, 1].reshape(n_date * cols, lines)

    ref_index = ref_date[0]
    ref_scale = scales[ref_index]
    ref_re = lax.dynamic_slice_in_dim(x_re, ref_index * cols, cols, 0).astype(f32) * ref_scale
    ref_im = lax.dynamic_slice_in_dim(x_im, ref_index * cols, cols, 0).astype(f32) * ref_scale
    ref_re = jnp.tile(ref_re, (n_date, 1))
    ref_im = jnp.tile(ref_im, (n_date, 1))
    row_scale = jnp.repeat(scales, cols)[:, None]
    a_re = x_re.astype(f32) * row_scale
    a_im = x_im.astype(f32) * row_scale
    ifg_re = (a_re * ref_re + a_im * ref_im).astype(jnp.bfloat16)
    ifg_im = (a_im * ref_re - a_re * ref_im).astype(jnp.bfloat16)

    cos_t, sin_t = dft_table(lines)
    rows = n_date * cols
    stacked = jnp.concatenate([ifg_re, ifg_im], axis=0)
    fc = jnp.dot(stacked, cos_t, preferred_element_type=f32)
    fs = jnp.dot(stacked, sin_t, preferred_element_type=f32)
    spec_re = fc[:rows] + fs[rows:]
    spec_im = fc[rows:] - fs[:rows]
    weights = gain[None, :]
    held = jnp.concatenate(
        [(spec_re * weights).astype(jnp.bfloat16), (spec_im * weights).astype(jnp.bfloat16)],
        axis=0,
    )
    bc = jnp.dot(held, cos_t, preferred_element_type=f32)
    bs = jnp.dot(held, sin_t, preferred_element_type=f32)
    filt_re = ((bc[:rows] - bs[rows:]) * (1.0 / lines)).astype(jnp.bfloat16)
    filt_im = ((bs[:rows] + bc[rows:]) * (1.0 / lines)).astype(jnp.bfloat16)

    pair = jnp.concatenate([filt_re, filt_im], axis=0).reshape(2, n_date, cols, lines)
    pair = pair.transpose(2, 0, 1, 3).reshape(2 * rows, lines).T
    got = lax.all_to_all(pair, "date", split_axis=0, concat_axis=0, tiled=True)
    z = got.reshape(n_date, lines_dev, cols, 2 * n_date).transpose(1, 2, 0, 3)
    z = z.reshape(lines_dev * cols * n_date, 2 * n_date)

    grid_size = HGRID * VGRID
    phase = phase_tables(bperp, tdays)
    spectra = jnp.dot(z, phase, preferred_element_type=f32)
    peri_re = spectra[:, :grid_size]
    peri_im = spectra[:, grid_size:]
    wide = z.astype(f32)
    pixel_power = jnp.sum(wide * wide, axis=1) / n_date
    mask_rows = lax.dynamic_slice_in_dim(mask, me * lines_dev, lines_dev, 0)
    mask_px = mask_rows.reshape(-1).astype(f32)
    result = (peri_re * peri_re + peri_im * peri_im) / (
        n_date * jnp.maximum(pixel_power, 1.0)
    )[:, None]
    result = result * mask_px[:, None]
    return result.reshape(lines_dev, cols * n_date, grid_size)


def solution(mesh):
    in_specs = (P("date", None, "rng"), P("date", None, "rng"), P(), P(), P(), P(), P(None, "rng"))
    out_specs = P("date", "rng", None)
    return jax.shard_map(shards, mesh=mesh, in_specs=in_specs, out_specs=out_specs, check_vma=False)
```

```python
import functools
import math

import jax
import jax.numpy as jnp
from jax import lax
from jax.experimental import pallas as pl
from jax.sharding import PartitionSpec as P

HGRID = 16
VGRID = 16
PHASE_Q = 1024


def dft_table(length):
    split = 64
    hi_count = length // split
    freq = jnp.arange(length, dtype=jnp.int32)[:, None]
    step = 2.0 * math.pi / length
    hi_ang = ((freq * (split * jnp.arange(hi_count, dtype=jnp.int32)[None, :])) % length).astype(
        jnp.float32
    ) * step
    lo_ang = ((freq * jnp.arange(split, dtype=jnp.int32)[None, :]) % length).astype(
        jnp.float32
    ) * step
    hi_c, hi_s = jnp.cos(hi_ang)[:, :, None], jnp.sin(hi_ang)[:, :, None]
    lo_c, lo_s = jnp.cos(lo_ang)[:, None, :], jnp.sin(lo_ang)[:, None, :]
    cos_t = (hi_c * lo_c - hi_s * lo_s).reshape(length, length).astype(jnp.bfloat16)
    sin_t = (hi_c * lo_s + hi_s * lo_c).reshape(length, length).astype(jnp.bfloat16)
    return lax.optimization_barrier((cos_t, sin_t))


def phase_tables(bperp, tdays):
    grid_points = jnp.arange(HGRID * VGRID, dtype=jnp.int32)
    height_step = grid_points // VGRID
    speed_step = grid_points % VGRID
    quanta = (
        bperp[:, None] * height_step[None, :] + tdays[:, None] * speed_step[None, :]
    ) % PHASE_Q
    angles = quanta.astype(jnp.float32) * (2.0 * math.pi / PHASE_Q)
    phase_re = jnp.cos(angles).astype(jnp.bfloat16)
    phase_im = jnp.sin(angles).astype(jnp.bfloat16)
    upper = jnp.concatenate([phase_re, -phase_im], axis=1)
    lower = jnp.concatenate([phase_im, phase_re], axis=1)
    return jnp.concatenate([upper, lower], axis=0)


def _tail_kernel(n_date, grid_size, z_ref, ph_ref, m_ref, o_ref):
    z = z_ref[...]
    spectra = jnp.dot(z, ph_ref[...], preferred_element_type=jnp.float32)
    peri_re = spectra[:, :grid_size]
    peri_im = spectra[:, grid_size:]
    wide = z.astype(jnp.float32)
    pixel_power = jnp.sum(wide * wide, axis=1, keepdims=True) / n_date
    val = (peri_re * peri_re + peri_im * peri_im) / (n_date * jnp.maximum(pixel_power, 1.0))
    o_ref[...] = val * m_ref[...]


def periodogram(z, phase, mask_px, n_date, block=512):
    rows, depth = z.shape
    grid_size = phase.shape[1] // 2
    return pl.pallas_call(
        functools.partial(_tail_kernel, n_date, grid_size),
        out_shape=jax.ShapeDtypeStruct((rows, grid_size), jnp.float32),
        grid=(rows // block,),
        in_specs=[
            pl.BlockSpec((block, depth), lambda i: (i, 0)),
            pl.BlockSpec(phase.shape, lambda i: (0, 0)),
            pl.BlockSpec((block, 1), lambda i: (i, 0)),
        ],
        out_specs=pl.BlockSpec((block, grid_size), lambda i: (i, 0)),
        cost_estimate=pl.CostEstimate(
            flops=2 * rows * depth * 2 * grid_size,
            transcendentals=0,
            bytes_accessed=rows * depth * 2 + rows * grid_size * 4 + rows * 4,
        ),
    )(z, phase, mask_px)


def shards(slc_re, slc_im, ref_date, gain, bperp, tdays, mask):
    date_dev, lines, rg_dev = slc_re.shape
    assert date_dev == 1
    n_date = lax.axis_size("date")
    n_rng = lax.axis_size("rng")
    cols = rg_dev // n_date
    lines_dev = lines // n_date
    pixel_total = lines * rg_dev * n_rng
    me = lax.axis_index("date")
    f32 = jnp.float32

    own_re = slc_re[0]
    own_im = slc_im[0]
    wide_re = own_re.astype(f32)
    wide_im = own_im.astype(f32)
    local = jnp.sum(wide_re * wide_re + wide_im * wide_im)
    rng_me = lax.axis_index("rng")
    received = [local] + [
        lax.ppermute(local, "rng", [(r, (r + k) % n_rng) for r in range(n_rng)])
        for k in range(1, n_rng)
    ]
    by_shift = jnp.stack(received)
    by_source = by_shift[(rng_me - jnp.arange(n_rng)) % n_rng]
    own_sum = by_source[0]
    for k in range(1, n_rng):
        own_sum = own_sum + by_source[k]
    lane = jnp.arange(128)
    word = jnp.where(lane < 3, own_sum, 0.0)
    hi = lax.reduce_precision(word, exponent_bits=8, mantissa_bits=7)
    mid = lax.reduce_precision(word - hi, exponent_bits=8, mantissa_bits=7)
    lo = lax.reduce_precision(word - hi - mid, exponent_bits=8, mantissa_bits=7)
    word = jnp.where(lane == 0, hi, jnp.where(lane == 1, mid, lo))
    word = jnp.broadcast_to(word.astype(jnp.bfloat16), (n_date, 2 * cols, 128))

    both = jnp.stack([own_re.T, own_im.T]).reshape(2, cols, n_date, lines)
    both = both.transpose(2, 0, 1, 3).reshape(n_date, 2 * cols, lines)
    both = jnp.concatenate([both, word], axis=2)
    got = lax.all_to_all(both, "date", split_axis=0, concat_axis=0, tiled=True)
    sums = got[:, 0, lines:lines + 3].astype(f32)
    date_sums = (sums[:, 0] + sums[:, 1]) + sums[:, 2]
    scales = lax.rsqrt(date_sums / pixel_total + 1e-06)
    got = got[:, :, :lines].reshape(n_date, 2, cols, lines)
    x_re = got[:, 0].reshape(n_date * cols, lines)
    x_im = got[:, 1].reshape(n_date * cols, lines)

    ref_index = ref_date[0]
    ref_scale = scales[ref_index]
    ref_re = lax.dynamic_slice_in_dim(x_re, ref_index * cols, cols, 0).astype(f32) * ref_scale
    ref_im = lax.dynamic_slice_in_dim(x_im, ref_index * cols, cols, 0).astype(f32) * ref_scale
    ref_re = jnp.tile(ref_re, (n_date, 1))
    ref_im = jnp.tile(ref_im, (n_date, 1))
    row_scale = jnp.repeat(scales, cols)[:, None]
    a_re = x_re.astype(f32) * row_scale
    a_im = x_im.astype(f32) * row_scale
    ifg_re = (a_re * ref_re + a_im * ref_im).astype(jnp.bfloat16)
    ifg_im = (a_im * ref_re - a_re * ref_im).astype(jnp.bfloat16)

    cos_t, sin_t = dft_table(lines)
    rows = n_date * cols
    stacked = jnp.concatenate([ifg_re, ifg_im], axis=0)
    fc = jnp.dot(stacked, cos_t, preferred_element_type=f32)
    fs = jnp.dot(stacked, sin_t, preferred_element_type=f32)
    spec_re = fc[:rows] + fs[rows:]
    spec_im = fc[rows:] - fs[:rows]
    weights = gain[None, :]
    held = jnp.concatenate(
        [(spec_re * weights).astype(jnp.bfloat16), (spec_im * weights).astype(jnp.bfloat16)],
        axis=0,
    )
    bc = jnp.dot(held, cos_t, preferred_element_type=f32)
    bs = jnp.dot(held, sin_t, preferred_element_type=f32)
    filt_re = ((bc[:rows] - bs[rows:]) * (1.0 / lines)).astype(jnp.bfloat16)
    filt_im = ((bs[:rows] + bc[rows:]) * (1.0 / lines)).astype(jnp.bfloat16)

    pair = jnp.concatenate([filt_re, filt_im], axis=0).reshape(2, n_date, cols, lines)
    pair = pair.transpose(2, 0, 1, 3).reshape(2 * rows, lines).T
    got = lax.all_to_all(pair, "date", split_axis=0, concat_axis=0, tiled=True)
    z = got.reshape(n_date, lines_dev, cols, 2 * n_date).transpose(1, 2, 0, 3)
    z = z.reshape(lines_dev * cols * n_date, 2 * n_date)

    phase = phase_tables(bperp, tdays)
    mask_rows = lax.dynamic_slice_in_dim(mask, me * lines_dev, lines_dev, 0)
    mask_px = mask_rows.reshape(-1, 1).astype(f32)
    result = periodogram(z, phase, mask_px, n_date)
    return result.reshape(lines_dev, cols * n_date, HGRID * VGRID)


def solution(mesh):
    in_specs = (P("date", None, "rng"), P("date", None, "rng"), P(), P(), P(), P(), P(None, "rng"))
    out_specs = P("date", "rng", None)
    return jax.shard_map(shards, mesh=mesh, in_specs=in_specs, out_specs=out_specs, check_vma=False)
```

```python
import functools
import math

import jax
import jax.numpy as jnp
from jax import lax
from jax.experimental import pallas as pl
from jax.sharding import PartitionSpec as P

HGRID = 16
VGRID = 16
PHASE_Q = 1024


def dft_table(length):
    split = 64
    hi_count = length // split
    freq = jnp.arange(length, dtype=jnp.int32)[:, None]
    step = 2.0 * math.pi / length
    hi_ang = ((freq * (split * jnp.arange(hi_count, dtype=jnp.int32)[None, :])) % length).astype(
        jnp.float32
    ) * step
    lo_ang = ((freq * jnp.arange(split, dtype=jnp.int32)[None, :]) % length).astype(
        jnp.float32
    ) * step
    hi_c, hi_s = jnp.cos(hi_ang)[:, :, None], jnp.sin(hi_ang)[:, :, None]
    lo_c, lo_s = jnp.cos(lo_ang)[:, None, :], jnp.sin(lo_ang)[:, None, :]
    cos_t = (hi_c * lo_c - hi_s * lo_s).reshape(length, length).astype(jnp.bfloat16)
    sin_t = (hi_c * lo_s + hi_s * lo_c).reshape(length, length).astype(jnp.bfloat16)
    return lax.optimization_barrier((cos_t, sin_t))


def phase_tables(bperp, tdays):
    grid_points = jnp.arange(HGRID * VGRID, dtype=jnp.int32)
    height_step = grid_points // VGRID
    speed_step = grid_points % VGRID
    quanta = (
        bperp[:, None] * height_step[None, :] + tdays[:, None] * speed_step[None, :]
    ) % PHASE_Q
    angles = quanta.astype(jnp.float32) * (2.0 * math.pi / PHASE_Q)
    phase_re = jnp.cos(angles).astype(jnp.bfloat16)
    phase_im = jnp.sin(angles).astype(jnp.bfloat16)
    upper = jnp.concatenate([phase_re, -phase_im], axis=1)
    lower = jnp.concatenate([phase_im, phase_re], axis=1)
    return jnp.concatenate([upper, lower], axis=0)


def _tail_kernel(n_date, grid_size, z_ref, ph_ref, m_ref, o_ref):
    z = z_ref[...]
    spectra = jnp.dot(z, ph_ref[...], preferred_element_type=jnp.float32)
    peri_re = spectra[:, :grid_size]
    peri_im = spectra[:, grid_size:]
    wide = z.astype(jnp.float32)
    pixel_power = jnp.sum(wide * wide, axis=1, keepdims=True) / n_date
    row_factor = m_ref[...] / (n_date * jnp.maximum(pixel_power, 1.0))
    o_ref[...] = (peri_re * peri_re + peri_im * peri_im) * row_factor


def periodogram(z, phase, mask_px, n_date, block=1024):
    rows, depth = z.shape
    grid_size = phase.shape[1] // 2
    return pl.pallas_call(
        functools.partial(_tail_kernel, n_date, grid_size),
        out_shape=jax.ShapeDtypeStruct((rows, grid_size), jnp.float32),
        grid=(rows // block,),
        in_specs=[
            pl.BlockSpec((block, depth), lambda i: (i, 0)),
            pl.BlockSpec(phase.shape, lambda i: (0, 0)),
            pl.BlockSpec((block, 1), lambda i: (i, 0)),
        ],
        out_specs=pl.BlockSpec((block, grid_size), lambda i: (i, 0)),
        cost_estimate=pl.CostEstimate(
            flops=2 * rows * depth * 2 * grid_size,
            transcendentals=0,
            bytes_accessed=rows * depth * 2 + rows * grid_size * 4 + rows * 4,
        ),
    )(z, phase, mask_px)


def shards(slc_re, slc_im, ref_date, gain, bperp, tdays, mask):
    date_dev, lines, rg_dev = slc_re.shape
    assert date_dev == 1
    n_date = lax.axis_size("date")
    n_rng = lax.axis_size("rng")
    cols = rg_dev // n_date
    lines_dev = lines // n_date
    pixel_total = lines * rg_dev * n_rng
    me = lax.axis_index("date")
    f32 = jnp.float32

    own_re = slc_re[0]
    own_im = slc_im[0]
    wide_re = own_re.astype(f32)
    wide_im = own_im.astype(f32)
    local = jnp.sum(wide_re * wide_re + wide_im * wide_im)
    rng_me = lax.axis_index("rng")
    received = [local] + [
        lax.ppermute(local, "rng", [(r, (r + k) % n_rng) for r in range(n_rng)])
        for k in range(1, n_rng)
    ]
    by_shift = jnp.stack(received)
    by_source = by_shift[(rng_me - jnp.arange(n_rng)) % n_rng]
    own_sum = by_source[0]
    for k in range(1, n_rng):
        own_sum = own_sum + by_source[k]
    lane = jnp.arange(128)
    word = jnp.where(lane < 3, own_sum, 0.0)
    hi = lax.reduce_precision(word, exponent_bits=8, mantissa_bits=7)
    mid = lax.reduce_precision(word - hi, exponent_bits=8, mantissa_bits=7)
    lo = lax.reduce_precision(word - hi - mid, exponent_bits=8, mantissa_bits=7)
    word = jnp.where(lane == 0, hi, jnp.where(lane == 1, mid, lo))
    word = jnp.broadcast_to(word.astype(jnp.bfloat16), (n_date, 2 * cols, 128))

    both = jnp.stack([own_re.T, own_im.T]).reshape(2, cols, n_date, lines)
    both = both.transpose(2, 0, 1, 3).reshape(n_date, 2 * cols, lines)
    both = jnp.concatenate([both, word], axis=2)
    got = lax.all_to_all(both, "date", split_axis=0, concat_axis=0, tiled=True)
    sums = got[:, 0, lines:lines + 3].astype(f32)
    date_sums = (sums[:, 0] + sums[:, 1]) + sums[:, 2]
    scales = lax.rsqrt(date_sums / pixel_total + 1e-06)
    got = got[:, :, :lines].reshape(n_date, 2, cols, lines)
    x_re = got[:, 0].reshape(n_date * cols, lines)
    x_im = got[:, 1].reshape(n_date * cols, lines)

    ref_index = ref_date[0]
    ref_scale = scales[ref_index]
    ref_re = lax.dynamic_slice_in_dim(x_re, ref_index * cols, cols, 0).astype(f32) * ref_scale
    ref_im = lax.dynamic_slice_in_dim(x_im, ref_index * cols, cols, 0).astype(f32) * ref_scale
    ref_re = jnp.tile(ref_re, (n_date, 1))
    ref_im = jnp.tile(ref_im, (n_date, 1))
    row_scale = jnp.repeat(scales, cols)[:, None]
    a_re = x_re.astype(f32) * row_scale
    a_im = x_im.astype(f32) * row_scale
    ifg_re = (a_re * ref_re + a_im * ref_im).astype(jnp.bfloat16)
    ifg_im = (a_im * ref_re - a_re * ref_im).astype(jnp.bfloat16)

    cos_t, sin_t = dft_table(lines)
    rows = n_date * cols
    stacked = jnp.concatenate([ifg_re, ifg_im], axis=0)
    fc = jnp.dot(stacked, cos_t, preferred_element_type=f32)
    fs = jnp.dot(stacked, sin_t, preferred_element_type=f32)
    spec_re = fc[:rows] + fs[rows:]
    spec_im = fc[rows:] - fs[:rows]
    weights = gain[None, :]
    held = jnp.concatenate(
        [(spec_re * weights).astype(jnp.bfloat16), (spec_im * weights).astype(jnp.bfloat16)],
        axis=0,
    )
    bc = jnp.dot(held, cos_t, preferred_element_type=f32)
    bs = jnp.dot(held, sin_t, preferred_element_type=f32)
    filt_re = ((bc[:rows] - bs[rows:]) * (1.0 / lines)).astype(jnp.bfloat16)
    filt_im = ((bs[:rows] + bc[rows:]) * (1.0 / lines)).astype(jnp.bfloat16)

    pair = jnp.concatenate([filt_re, filt_im], axis=0).reshape(2, n_date, cols, lines)
    pair = pair.transpose(2, 0, 1, 3).reshape(2 * rows, lines).T
    got = lax.all_to_all(pair, "date", split_axis=0, concat_axis=0, tiled=True)
    z = got.reshape(n_date, lines_dev, cols, 2 * n_date).transpose(1, 2, 0, 3)
    z = z.reshape(lines_dev * cols * n_date, 2 * n_date)

    phase = phase_tables(bperp, tdays)
    mask_rows = lax.dynamic_slice_in_dim(mask, me * lines_dev, lines_dev, 0)
    mask_px = mask_rows.reshape(-1, 1).astype(f32)
    result = periodogram(z, phase, mask_px, n_date)
    return result.reshape(lines_dev, cols * n_date, HGRID * VGRID)


def solution(mesh):
    in_specs = (P("date", None, "rng"), P("date", None, "rng"), P(), P(), P(), P(), P(None, "rng"))
    out_specs = P("date", "rng", None)
    return jax.shard_map(shards, mesh=mesh, in_specs=in_specs, out_specs=out_specs, check_vma=False)
```

```python
import math

import jax
import jax.numpy as jnp
from jax import lax
from jax.sharding import PartitionSpec as P

HGRID = 16
VGRID = 16
PHASE_Q = 1024


def wave_table(length, freqs):
    split = 32
    hi_count = length // split
    step = 2.0 * math.pi / length
    cols = freqs[None, :]
    hi_ang = ((split * jnp.arange(hi_count, dtype=jnp.int32)[:, None] * cols) % length).astype(
        jnp.float32
    ) * step
    lo_ang = ((jnp.arange(split, dtype=jnp.int32)[:, None] * cols) % length).astype(
        jnp.float32
    ) * step
    hi_c, hi_s = jnp.cos(hi_ang)[:, None, :], jnp.sin(hi_ang)[:, None, :]
    lo_c, lo_s = jnp.cos(lo_ang)[None, :, :], jnp.sin(lo_ang)[None, :, :]
    count = freqs.shape[0]
    cos_t = (hi_c * lo_c - hi_s * lo_s).reshape(length, count).astype(jnp.bfloat16)
    sin_t = (hi_c * lo_s + hi_s * lo_c).reshape(length, count).astype(jnp.bfloat16)
    return cos_t, sin_t


def phase_tables(bperp, tdays):
    grid_points = jnp.arange(HGRID * VGRID, dtype=jnp.int32)
    height_step = grid_points // VGRID
    speed_step = grid_points % VGRID
    quanta = (
        bperp[:, None] * height_step[None, :] + tdays[:, None] * speed_step[None, :]
    ) % PHASE_Q
    angles = quanta.astype(jnp.float32) * (2.0 * math.pi / PHASE_Q)
    phase_re = jnp.cos(angles).astype(jnp.bfloat16)
    phase_im = jnp.sin(angles).astype(jnp.bfloat16)
    upper = jnp.concatenate([phase_re, -phase_im], axis=1)
    lower = jnp.concatenate([phase_im, phase_re], axis=1)
    return jnp.concatenate([upper, lower], axis=0)


def shards(slc_re, slc_im, ref_date, gain, bperp, tdays, mask):
    date_dev, lines, rg_dev = slc_re.shape
    assert date_dev == 1
    n_date = lax.axis_size("date")
    n_rng = lax.axis_size("rng")
    cols = rg_dev // n_date
    lines_dev = lines // n_date
    pixel_total = lines * rg_dev * n_rng
    me = lax.axis_index("date")
    f32 = jnp.float32

    own_re = slc_re[0]
    own_im = slc_im[0]
    wide_re = own_re.astype(f32)
    wide_im = own_im.astype(f32)
    local = jnp.sum(wide_re * wide_re + wide_im * wide_im)
    rng_me = lax.axis_index("rng")
    received = [local] + [
        lax.ppermute(local, "rng", [(r, (r + k) % n_rng) for r in range(n_rng)])
        for k in range(1, n_rng)
    ]
    by_shift = jnp.stack(received)
    by_source = by_shift[(rng_me - jnp.arange(n_rng)) % n_rng]
    own_sum = by_source[0]
    for k in range(1, n_rng):
        own_sum = own_sum + by_source[k]
    lane = jnp.arange(128)
    word = jnp.where(lane < 3, own_sum, 0.0)
    hi = lax.reduce_precision(word, exponent_bits=8, mantissa_bits=7)
    mid = lax.reduce_precision(word - hi, exponent_bits=8, mantissa_bits=7)
    lo = lax.reduce_precision(word - hi - mid, exponent_bits=8, mantissa_bits=7)
    word = jnp.where(lane == 0, hi, jnp.where(lane == 1, mid, lo))
    word = jnp.broadcast_to(word.astype(jnp.bfloat16), (n_date, 2 * cols, 128))

    half = lines // 2
    split_re = own_re.reshape(half, 2, rg_dev).transpose(1, 0, 2).reshape(lines, rg_dev)
    split_im = own_im.reshape(half, 2, rg_dev).transpose(1, 0, 2).reshape(lines, rg_dev)
    both = jnp.stack([split_re.T, split_im.T]).reshape(2, cols, n_date, lines)
    both = both.transpose(2, 0, 1, 3).reshape(n_date, 2 * cols, lines)
    both = jnp.concatenate([both, word], axis=2)
    got = lax.all_to_all(both, "date", split_axis=0, concat_axis=0, tiled=True)
    sums = got[:, 0, lines:lines + 3].astype(f32)
    date_sums = (sums[:, 0] + sums[:, 1]) + sums[:, 2]
    scales = lax.rsqrt(date_sums / pixel_total + 1e-06)
    got = got[:, :, :lines].reshape(n_date, 2, cols, lines)
    x_re = got[:, 0].reshape(n_date * cols, lines)
    x_im = got[:, 1].reshape(n_date * cols, lines)

    ref_index = ref_date[0]
    ref_scale = scales[ref_index]
    ref_re = lax.dynamic_slice_in_dim(x_re, ref_index * cols, cols, 0).astype(f32) * ref_scale
    ref_im = lax.dynamic_slice_in_dim(x_im, ref_index * cols, cols, 0).astype(f32) * ref_scale
    ref_re = jnp.tile(ref_re, (n_date, 1))
    ref_im = jnp.tile(ref_im, (n_date, 1))
    row_scale = jnp.repeat(scales, cols)[:, None]
    a_re = x_re.astype(f32) * row_scale
    a_im = x_im.astype(f32) * row_scale
    ifg_re = (a_re * ref_re + a_im * ref_im).astype(jnp.bfloat16)
    ifg_im = (a_im * ref_re - a_re * ref_im).astype(jnp.bfloat16)

    rows = n_date * cols
    quarter = half // 2
    freq_order = jnp.concatenate(
        [jnp.arange(0, half, 2, dtype=jnp.int32), jnp.arange(1, half, 2, dtype=jnp.int32)]
    )
    fwd_cos, fwd_sin = wave_table(half, freq_order)
    inv_cos, inv_sin = wave_table(half, jnp.arange(half, dtype=jnp.int32))
    fwd_cos, fwd_sin, inv_cos, inv_sin = lax.optimization_barrier(
        (fwd_cos, fwd_sin, inv_cos, inv_sin)
    )
    fwd_ang = freq_order.astype(f32) * (2.0 * math.pi / lines)
    inv_ang = jnp.arange(half, dtype=f32) * (2.0 * math.pi / lines)

    def half_dft(x_even, x_odd, tab_cos, tab_sin, sign):
        def one(x):
            pc = jnp.dot(x, tab_cos, preferred_element_type=f32)
            ps = jnp.dot(x, tab_sin, preferred_element_type=f32)
            if sign < 0:
                return pc[:rows] + ps[rows:], pc[rows:] - ps[:rows]
            return pc[:rows] - ps[rows:], ps[:rows] + pc[rows:]

        e_re, e_im = one(x_even)
        o_re, o_im = one(x_odd)
        ang = fwd_ang if sign < 0 else inv_ang
        tw_re = jnp.cos(ang)[None, :]
        tw_im = (sign * jnp.sin(ang))[None, :]
        t_re = o_re * tw_re - o_im * tw_im
        t_im = o_re * tw_im + o_im * tw_re
        return (e_re + t_re, e_im + t_im), (e_re - t_re, e_im - t_im)

    stacked = jnp.concatenate([ifg_re, ifg_im], axis=0)
    (lo_re, lo_im), (hi_re, hi_im) = half_dft(
        stacked[:, :half], stacked[:, half:], fwd_cos, fwd_sin, -1
    )
    spec_e_re = jnp.concatenate([lo_re[:, :quarter], hi_re[:, :quarter]], axis=1)
    spec_e_im = jnp.concatenate([lo_im[:, :quarter], hi_im[:, :quarter]], axis=1)
    spec_o_re = jnp.concatenate([lo_re[:, quarter:], hi_re[:, quarter:]], axis=1)
    spec_o_im = jnp.concatenate([lo_im[:, quarter:], hi_im[:, quarter:]], axis=1)
    gain_pairs = gain.reshape(half, 2)
    w_e = gain_pairs[:, 0][None, :]
    w_o = gain_pairs[:, 1][None, :]
    held_e = jnp.concatenate(
        [(spec_e_re * w_e).astype(jnp.bfloat16), (spec_e_im * w_e).astype(jnp.bfloat16)], axis=0
    )
    held_o = jnp.concatenate(
        [(spec_o_re * w_o).astype(jnp.bfloat16), (spec_o_im * w_o).astype(jnp.bfloat16)], axis=0
    )
    (a_re, a_im), (b_re, b_im) = half_dft(held_e, held_o, inv_cos, inv_sin, 1)
    filt_re = (jnp.concatenate([a_re, b_re], axis=1) * (1.0 / lines)).astype(jnp.bfloat16)
    filt_im = (jnp.concatenate([a_im, b_im], axis=1) * (1.0 / lines)).astype(jnp.bfloat16)

    pair = jnp.concatenate([filt_re, filt_im], axis=0).reshape(2, n_date, cols, lines)
    pair = pair.transpose(2, 0, 1, 3).reshape(2 * rows, lines).T
    got = lax.all_to_all(pair, "date", split_axis=0, concat_axis=0, tiled=True)
    z = got.reshape(n_date, lines_dev, cols, 2 * n_date).transpose(1, 2, 0, 3)
    z = z.reshape(lines_dev * cols * n_date, 2 * n_date)

    grid_size = HGRID * VGRID
    phase = phase_tables(bperp, tdays)
    spectra = jnp.dot(z, phase, preferred_element_type=f32)
    peri_re = spectra[:, :grid_size]
    peri_im = spectra[:, grid_size:]
    wide = z.astype(f32)
    pixel_power = jnp.sum(wide * wide, axis=1) / n_date
    mask_rows = lax.dynamic_slice_in_dim(mask, me * lines_dev, lines_dev, 0)
    mask_px = mask_rows.reshape(-1).astype(f32)
    result = (peri_re * peri_re + peri_im * peri_im) / (
        n_date * jnp.maximum(pixel_power, 1.0)
    )[:, None]
    result = result * mask_px[:, None]
    return result.reshape(lines_dev, cols * n_date, grid_size)


def solution(mesh):
    in_specs = (P("date", None, "rng"), P("date", None, "rng"), P(), P(), P(), P(), P(None, "rng"))
    out_specs = P("date", "rng", None)
    return jax.shard_map(shards, mesh=mesh, in_specs=in_specs, out_specs=out_specs, check_vma=False)
```

```python
import math

import jax
import jax.numpy as jnp
from jax import lax
from jax.sharding import PartitionSpec as P

HGRID = 16
VGRID = 16
PHASE_Q = 1024


def dft_table(length):
    split = 64
    hi_count = length // split
    freq = jnp.arange(length, dtype=jnp.int32)[:, None]
    step = 2.0 * math.pi / length
    hi_ang = ((freq * (split * jnp.arange(hi_count, dtype=jnp.int32)[None, :])) % length).astype(
        jnp.float32
    ) * step
    lo_ang = ((freq * jnp.arange(split, dtype=jnp.int32)[None, :]) % length).astype(
        jnp.float32
    ) * step
    hi_c, hi_s = jnp.cos(hi_ang)[:, :, None], jnp.sin(hi_ang)[:, :, None]
    lo_c, lo_s = jnp.cos(lo_ang)[:, None, :], jnp.sin(lo_ang)[:, None, :]
    cos_t = (hi_c * lo_c - hi_s * lo_s).reshape(length, length).astype(jnp.bfloat16)
    sin_t = (hi_c * lo_s + hi_s * lo_c).reshape(length, length).astype(jnp.bfloat16)
    return lax.optimization_barrier((cos_t, sin_t))


def phase_tables(bperp, tdays):
    grid_points = jnp.arange(HGRID * VGRID, dtype=jnp.int32)
    height_step = grid_points // VGRID
    speed_step = grid_points % VGRID
    quanta = (
        bperp[:, None] * height_step[None, :] + tdays[:, None] * speed_step[None, :]
    ) % PHASE_Q
    angles = quanta.astype(jnp.float32) * (2.0 * math.pi / PHASE_Q)
    phase_re = jnp.cos(angles).astype(jnp.bfloat16)
    phase_im = jnp.sin(angles).astype(jnp.bfloat16)
    upper = jnp.concatenate([phase_re, -phase_im], axis=1)
    lower = jnp.concatenate([phase_im, phase_re], axis=1)
    return jnp.concatenate([upper, lower], axis=0)


def shards(slc_re, slc_im, ref_date, gain, bperp, tdays, mask):
    date_dev, lines, rg_dev = slc_re.shape
    assert date_dev == 1
    n_date = lax.axis_size("date")
    n_rng = lax.axis_size("rng")
    cols = rg_dev // n_date
    lines_dev = lines // n_date
    pixel_total = lines * rg_dev * n_rng
    me = lax.axis_index("date")
    f32 = jnp.float32

    own_re = slc_re[0]
    own_im = slc_im[0]
    wide_re = own_re.astype(f32)
    wide_im = own_im.astype(f32)
    local = jnp.sum(wide_re * wide_re + wide_im * wide_im)
    own_sum = local
    for k in range(1, n_rng):
        own_sum = own_sum + lax.ppermute(
            local, "rng", [(r, (r + k) % n_rng) for r in range(n_rng)]
        )
    lane = jnp.arange(128)
    word = jnp.where(lane < 3, own_sum, 0.0)
    hi = lax.reduce_precision(word, exponent_bits=8, mantissa_bits=7)
    mid = lax.reduce_precision(word - hi, exponent_bits=8, mantissa_bits=7)
    lo = lax.reduce_precision(word - hi - mid, exponent_bits=8, mantissa_bits=7)
    word = jnp.where(lane == 0, hi, jnp.where(lane == 1, mid, lo))
    word = jnp.broadcast_to(word.astype(jnp.bfloat16), (n_date, 2 * cols, 128))

    both = jnp.stack([own_re.T, own_im.T]).reshape(2, cols, n_date, lines)
    both = both.transpose(2, 0, 1, 3).reshape(n_date, 2 * cols, lines)
    both = jnp.concatenate([both, word], axis=2)
    got = lax.all_to_all(both, "date", split_axis=0, concat_axis=0, tiled=True)
    sums = got[:, 0, lines:lines + 3].astype(f32)
    date_sums = (sums[:, 0] + sums[:, 1]) + sums[:, 2]
    scales = lax.rsqrt(date_sums / pixel_total + 1e-06)
    got = got[:, :, :lines].reshape(n_date, 2, cols, lines)
    x_re = got[:, 0].reshape(n_date * cols, lines)
    x_im = got[:, 1].reshape(n_date * cols, lines)

    ref_index = ref_date[0]
    ref_scale = scales[ref_index]
    ref_re = lax.dynamic_slice_in_dim(x_re, ref_index * cols, cols, 0).astype(f32) * ref_scale
    ref_im = lax.dynamic_slice_in_dim(x_im, ref_index * cols, cols, 0).astype(f32) * ref_scale
    ref_re = jnp.tile(ref_re, (n_date, 1))
    ref_im = jnp.tile(ref_im, (n_date, 1))
    row_scale = jnp.repeat(scales, cols)[:, None]
    a_re = x_re.astype(f32) * row_scale
    a_im = x_im.astype(f32) * row_scale
    ifg_re = (a_re * ref_re + a_im * ref_im).astype(jnp.bfloat16)
    ifg_im = (a_im * ref_re - a_re * ref_im).astype(jnp.bfloat16)

    cos_t, sin_t = dft_table(lines)
    rows = n_date * cols
    stacked = jnp.concatenate([ifg_re, ifg_im], axis=0)
    fc = jnp.dot(stacked, cos_t, preferred_element_type=f32)
    fs = jnp.dot(stacked, sin_t, preferred_element_type=f32)
    spec_re = fc[:rows] + fs[rows:]
    spec_im = fc[rows:] - fs[:rows]
    weights = gain[None, :]
    held = jnp.concatenate(
        [(spec_re * weights).astype(jnp.bfloat16), (spec_im * weights).astype(jnp.bfloat16)],
        axis=0,
    )
    bc = jnp.dot(held, cos_t, preferred_element_type=f32)
    bs = jnp.dot(held, sin_t, preferred_element_type=f32)
    filt_re = ((bc[:rows] - bs[rows:]) * (1.0 / lines)).astype(jnp.bfloat16)
    filt_im = ((bs[:rows] + bc[rows:]) * (1.0 / lines)).astype(jnp.bfloat16)

    pair = jnp.concatenate([filt_re, filt_im], axis=0).reshape(2, n_date, cols, lines)
    pair = pair.transpose(2, 0, 1, 3).reshape(2 * rows, lines).T
    got = lax.all_to_all(pair, "date", split_axis=0, concat_axis=0, tiled=True)
    z = got.reshape(n_date, lines_dev, cols, 2 * n_date).transpose(1, 2, 0, 3)
    z = z.reshape(lines_dev * cols * n_date, 2 * n_date)

    grid_size = HGRID * VGRID
    phase = phase_tables(bperp, tdays)
    spectra = jnp.dot(z, phase, preferred_element_type=f32)
    peri_re = spectra[:, :grid_size]
    peri_im = spectra[:, grid_size:]
    wide = z.astype(f32)
    pixel_power = jnp.sum(wide * wide, axis=1) / n_date
    mask_rows = lax.dynamic_slice_in_dim(mask, me * lines_dev, lines_dev, 0)
    mask_px = mask_rows.reshape(-1).astype(f32)
    result = (peri_re * peri_re + peri_im * peri_im) / (
        n_date * jnp.maximum(pixel_power, 1.0)
    )[:, None]
    result = result * mask_px[:, None]
    return result.reshape(lines_dev, cols * n_date, grid_size)


def solution(mesh):
    in_specs = (P("date", None, "rng"), P("date", None, "rng"), P(), P(), P(), P(), P(None, "rng"))
    out_specs = P("date", "rng", None)
    return jax.shard_map(shards, mesh=mesh, in_specs=in_specs, out_specs=out_specs, check_vma=False)
```

```python
import math

import jax
import jax.numpy as jnp
from jax import lax
from jax.sharding import PartitionSpec as P

HGRID = 16
VGRID = 16
PHASE_Q = 1024


def dft_table(length):
    split = 64
    hi_count = length // split
    freq = jnp.arange(length, dtype=jnp.int32)[:, None]
    step = 2.0 * math.pi / length
    hi_ang = ((freq * (split * jnp.arange(hi_count, dtype=jnp.int32)[None, :])) % length).astype(
        jnp.float32
    ) * step
    lo_ang = ((freq * jnp.arange(split, dtype=jnp.int32)[None, :]) % length).astype(
        jnp.float32
    ) * step
    hi_c, hi_s = jnp.cos(hi_ang)[:, :, None], jnp.sin(hi_ang)[:, :, None]
    lo_c, lo_s = jnp.cos(lo_ang)[:, None, :], jnp.sin(lo_ang)[:, None, :]
    cos_t = (hi_c * lo_c - hi_s * lo_s).reshape(length, length).astype(jnp.bfloat16)
    sin_t = (hi_c * lo_s + hi_s * lo_c).reshape(length, length).astype(jnp.bfloat16)
    return lax.optimization_barrier((cos_t, sin_t))


def phase_tables(bperp, tdays):
    grid_points = jnp.arange(HGRID * VGRID, dtype=jnp.int32)
    height_step = grid_points // VGRID
    speed_step = grid_points % VGRID
    quanta = (
        bperp[:, None] * height_step[None, :] + tdays[:, None] * speed_step[None, :]
    ) % PHASE_Q
    angles = quanta.astype(jnp.float32) * (2.0 * math.pi / PHASE_Q)
    phase_re = jnp.cos(angles).astype(jnp.bfloat16)
    phase_im = jnp.sin(angles).astype(jnp.bfloat16)
    upper = jnp.concatenate([phase_re, -phase_im], axis=1)
    lower = jnp.concatenate([phase_im, phase_re], axis=1)
    return jnp.concatenate([upper, lower], axis=0)


def shards(slc_re, slc_im, ref_date, gain, bperp, tdays, mask):
    date_dev, lines, rg_dev = slc_re.shape
    assert date_dev == 1
    n_date = lax.axis_size("date")
    n_rng = lax.axis_size("rng")
    cols = rg_dev // n_date
    lines_dev = lines // n_date
    pixel_total = lines * rg_dev * n_rng
    me = lax.axis_index("date")
    f32 = jnp.float32

    own_re = slc_re[0]
    own_im = slc_im[0]
    wide_re = own_re.astype(f32)
    wide_im = own_im.astype(f32)
    local = jnp.sum(wide_re * wide_re + wide_im * wide_im)
    own_sum = local
    for k in range(1, n_rng):
        own_sum = own_sum + lax.ppermute(
            local, "rng", [(r, (r + k) % n_rng) for r in range(n_rng)]
        )
    lane = jnp.arange(128)
    word = jnp.where(lane < 3, own_sum, 0.0)
    hi = lax.reduce_precision(word, exponent_bits=8, mantissa_bits=7)
    mid = lax.reduce_precision(word - hi, exponent_bits=8, mantissa_bits=7)
    lo = lax.reduce_precision(word - hi - mid, exponent_bits=8, mantissa_bits=7)
    word = jnp.where(lane == 0, hi, jnp.where(lane == 1, mid, lo))
    word = jnp.broadcast_to(word.astype(jnp.bfloat16), (n_date, 2 * cols, 128))

    both = jnp.stack([own_re.T, own_im.T]).reshape(2, cols, n_date, lines)
    both = both.transpose(2, 0, 1, 3).reshape(n_date, 2 * cols, lines)
    both = jnp.concatenate([both, word], axis=2)
    got = lax.all_to_all(both, "date", split_axis=0, concat_axis=0, tiled=True)
    sums = got[:, 0, lines:lines + 3].astype(f32)
    date_sums = (sums[:, 0] + sums[:, 1]) + sums[:, 2]
    scales = lax.rsqrt(date_sums / pixel_total + 1e-06)
    got = got[:, :, :lines].reshape(n_date, 2, cols, lines)
    x_re = got[:, 0].reshape(n_date * cols, lines)
    x_im = got[:, 1].reshape(n_date * cols, lines)

    ref_index = ref_date[0]
    ref_scale = scales[ref_index]
    rows = n_date * cols
    row_id = jnp.arange(rows, dtype=jnp.int32)[:, None]
    col_id = jnp.arange(rows, dtype=jnp.int32)[None, :]
    pick = (col_id == ref_index * cols + row_id % cols).astype(jnp.bfloat16)
    ref_re = jnp.dot(pick, x_re, preferred_element_type=f32) * ref_scale
    ref_im = jnp.dot(pick, x_im, preferred_element_type=f32) * ref_scale
    row_scale = jnp.repeat(scales, cols)[:, None]
    a_re = x_re.astype(f32) * row_scale
    a_im = x_im.astype(f32) * row_scale
    ifg_re = (a_re * ref_re + a_im * ref_im).astype(jnp.bfloat16)
    ifg_im = (a_im * ref_re - a_re * ref_im).astype(jnp.bfloat16)

    cos_t, sin_t = dft_table(lines)
    rows = n_date * cols
    stacked = jnp.concatenate([ifg_re, ifg_im], axis=0)
    fc = jnp.dot(stacked, cos_t, preferred_element_type=f32)
    fs = jnp.dot(stacked, sin_t, preferred_element_type=f32)
    spec_re = fc[:rows] + fs[rows:]
    spec_im = fc[rows:] - fs[:rows]
    weights = gain[None, :]
    held = jnp.concatenate(
        [(spec_re * weights).astype(jnp.bfloat16), (spec_im * weights).astype(jnp.bfloat16)],
        axis=0,
    )
    bc = jnp.dot(held, cos_t, preferred_element_type=f32)
    bs = jnp.dot(held, sin_t, preferred_element_type=f32)
    filt_re = ((bc[:rows] - bs[rows:]) * (1.0 / lines)).astype(jnp.bfloat16)
    filt_im = ((bs[:rows] + bc[rows:]) * (1.0 / lines)).astype(jnp.bfloat16)

    pair = jnp.concatenate([filt_re, filt_im], axis=0).reshape(2, n_date, cols, lines)
    pair = pair.transpose(2, 0, 1, 3).reshape(2 * rows, lines).T
    got = lax.all_to_all(pair, "date", split_axis=0, concat_axis=0, tiled=True)
    z = got.reshape(n_date, lines_dev, cols, 2 * n_date).transpose(1, 2, 0, 3)
    z = z.reshape(lines_dev * cols * n_date, 2 * n_date)

    grid_size = HGRID * VGRID
    phase = phase_tables(bperp, tdays)
    spectra = jnp.dot(z, phase, preferred_element_type=f32)
    peri_re = spectra[:, :grid_size]
    peri_im = spectra[:, grid_size:]
    wide = z.astype(f32)
    pixel_power = jnp.sum(wide * wide, axis=1) / n_date
    mask_rows = lax.dynamic_slice_in_dim(mask, me * lines_dev, lines_dev, 0)
    mask_px = mask_rows.reshape(-1).astype(f32)
    result = (peri_re * peri_re + peri_im * peri_im) / (
        n_date * jnp.maximum(pixel_power, 1.0)
    )[:, None]
    result = result * mask_px[:, None]
    return result.reshape(lines_dev, cols * n_date, grid_size)


def solution(mesh):
    in_specs = (P("date", None, "rng"), P("date", None, "rng"), P(), P(), P(), P(), P(None, "rng"))
    out_specs = P("date", "rng", None)
    return jax.shard_map(shards, mesh=mesh, in_specs=in_specs, out_specs=out_specs, check_vma=False)
```

```python
import math

import jax
import jax.numpy as jnp
from jax import lax
from jax.sharding import PartitionSpec as P

HGRID = 16
VGRID = 16
PHASE_Q = 1024


def dft_table(length):
    split = 64
    hi_count = length // split
    freq = jnp.arange(length, dtype=jnp.int32)[:, None]
    step = 2.0 * math.pi / length
    hi_ang = ((freq * (split * jnp.arange(hi_count, dtype=jnp.int32)[None, :])) % length).astype(
        jnp.float32
    ) * step
    lo_ang = ((freq * jnp.arange(split, dtype=jnp.int32)[None, :]) % length).astype(
        jnp.float32
    ) * step
    hi_c, hi_s = jnp.cos(hi_ang)[:, :, None], jnp.sin(hi_ang)[:, :, None]
    lo_c, lo_s = jnp.cos(lo_ang)[:, None, :], jnp.sin(lo_ang)[:, None, :]
    cos_t = (hi_c * lo_c - hi_s * lo_s).reshape(length, length).astype(jnp.bfloat16)
    sin_t = (hi_c * lo_s + hi_s * lo_c).reshape(length, length).astype(jnp.bfloat16)
    return lax.optimization_barrier((cos_t, sin_t))


def phase_tables(bperp, tdays):
    grid_points = jnp.arange(HGRID * VGRID, dtype=jnp.int32)
    height_step = grid_points // VGRID
    speed_step = grid_points % VGRID
    quanta = (
        bperp[:, None] * height_step[None, :] + tdays[:, None] * speed_step[None, :]
    ) % PHASE_Q
    angles = quanta.astype(jnp.float32) * (2.0 * math.pi / PHASE_Q)
    phase_re = jnp.cos(angles).astype(jnp.bfloat16)
    phase_im = jnp.sin(angles).astype(jnp.bfloat16)
    upper = jnp.concatenate([phase_re, -phase_im], axis=1)
    lower = jnp.concatenate([phase_im, phase_re], axis=1)
    return jnp.concatenate([upper, lower], axis=0)


def shards(slc_re, slc_im, ref_date, gain, bperp, tdays, mask):
    date_dev, lines, rg_dev = slc_re.shape
    assert date_dev == 1
    n_date = lax.axis_size("date")
    n_rng = lax.axis_size("rng")
    cols = rg_dev // n_date
    lines_dev = lines // n_date
    pixel_total = lines * rg_dev * n_rng
    me = lax.axis_index("date")
    f32 = jnp.float32

    own_re = slc_re[0]
    own_im = slc_im[0]
    wide_re = own_re.astype(f32)
    wide_im = own_im.astype(f32)
    local = jnp.sum(wide_re * wide_re + wide_im * wide_im)
    own_sum = local
    for k in range(1, n_rng):
        own_sum = own_sum + lax.ppermute(
            local, "rng", [(r, (r + k) % n_rng) for r in range(n_rng)]
        )
    lane = jnp.arange(128)
    word = jnp.where(lane < 3, own_sum, 0.0)
    hi = lax.reduce_precision(word, exponent_bits=8, mantissa_bits=7)
    mid = lax.reduce_precision(word - hi, exponent_bits=8, mantissa_bits=7)
    lo = lax.reduce_precision(word - hi - mid, exponent_bits=8, mantissa_bits=7)
    word = jnp.where(lane == 0, hi, jnp.where(lane == 1, mid, lo))
    word = jnp.broadcast_to(word.astype(jnp.bfloat16), (n_date, 2 * cols, 128))

    both = jnp.stack([own_re.T, own_im.T]).reshape(2, cols, n_date, lines)
    both = both.transpose(2, 0, 1, 3).reshape(n_date, 2 * cols, lines)
    both = jnp.concatenate([both, word], axis=2)
    got = lax.all_to_all(both, "date", split_axis=0, concat_axis=0, tiled=True)
    sums = got[:, 0, lines:lines + 3].astype(f32)
    date_sums = (sums[:, 0] + sums[:, 1]) + sums[:, 2]
    scales = lax.rsqrt(date_sums / pixel_total + 1e-06)
    ref_index = ref_date[0]
    ref_scale = scales[ref_index]
    rows = n_date * cols
    flat = got.reshape(n_date * 2 * cols, lines + 128)
    row_id = jnp.arange(rows, dtype=jnp.int32)[:, None]
    col_id = jnp.arange(n_date * 2 * cols, dtype=jnp.int32)[None, :]
    base = ref_index * 2 * cols + row_id % cols
    pick_re = (col_id == base).astype(jnp.bfloat16)
    pick_im = (col_id == base + cols).astype(jnp.bfloat16)
    ref_re = jnp.dot(pick_re, flat, preferred_element_type=f32)[:, :lines] * ref_scale
    ref_im = jnp.dot(pick_im, flat, preferred_element_type=f32)[:, :lines] * ref_scale
    x_re = got[:, :cols, :lines].reshape(rows, lines)
    x_im = got[:, cols:, :lines].reshape(rows, lines)
    row_scale = jnp.repeat(scales, cols)[:, None]
    a_re = x_re.astype(f32) * row_scale
    a_im = x_im.astype(f32) * row_scale
    ifg_re = (a_re * ref_re + a_im * ref_im).astype(jnp.bfloat16)
    ifg_im = (a_im * ref_re - a_re * ref_im).astype(jnp.bfloat16)

    cos_t, sin_t = dft_table(lines)
    rows = n_date * cols
    stacked = jnp.concatenate([ifg_re, ifg_im], axis=0)
    fc = jnp.dot(stacked, cos_t, preferred_element_type=f32)
    fs = jnp.dot(stacked, sin_t, preferred_element_type=f32)
    spec_re = fc[:rows] + fs[rows:]
    spec_im = fc[rows:] - fs[:rows]
    weights = gain[None, :]
    held = jnp.concatenate(
        [(spec_re * weights).astype(jnp.bfloat16), (spec_im * weights).astype(jnp.bfloat16)],
        axis=0,
    )
    bc = jnp.dot(held, cos_t, preferred_element_type=f32)
    bs = jnp.dot(held, sin_t, preferred_element_type=f32)
    filt_re = ((bc[:rows] - bs[rows:]) * (1.0 / lines)).astype(jnp.bfloat16)
    filt_im = ((bs[:rows] + bc[rows:]) * (1.0 / lines)).astype(jnp.bfloat16)

    pair = jnp.concatenate([filt_re, filt_im], axis=0).reshape(2, n_date, cols, lines)
    pair = pair.transpose(2, 0, 1, 3).reshape(2 * rows, lines).T
    got = lax.all_to_all(pair, "date", split_axis=0, concat_axis=0, tiled=True)
    z = got.reshape(n_date, lines_dev, cols, 2 * n_date).transpose(1, 2, 0, 3)
    z = z.reshape(lines_dev * cols * n_date, 2 * n_date)

    grid_size = HGRID * VGRID
    phase = phase_tables(bperp, tdays)
    spectra = jnp.dot(z, phase, preferred_element_type=f32)
    peri_re = spectra[:, :grid_size]
    peri_im = spectra[:, grid_size:]
    wide = z.astype(f32)
    pixel_power = jnp.sum(wide * wide, axis=1) / n_date
    mask_rows = lax.dynamic_slice_in_dim(mask, me * lines_dev, lines_dev, 0)
    mask_px = mask_rows.reshape(-1).astype(f32)
    result = (peri_re * peri_re + peri_im * peri_im) / (
        n_date * jnp.maximum(pixel_power, 1.0)
    )[:, None]
    result = result * mask_px[:, None]
    return result.reshape(lines_dev, cols * n_date, grid_size)


def solution(mesh):
    in_specs = (P("date", None, "rng"), P("date", None, "rng"), P(), P(), P(), P(), P(None, "rng"))
    out_specs = P("date", "rng", None)
    return jax.shard_map(shards, mesh=mesh, in_specs=in_specs, out_specs=out_specs, check_vma=False)
```

```python
import math

import jax
import jax.numpy as jnp
from jax import lax
from jax.sharding import PartitionSpec as P

HGRID = 16
VGRID = 16
PHASE_Q = 1024


def dft_table(length):
    split = 64
    hi_count = length // split
    freq = jnp.arange(length, dtype=jnp.int32)[:, None]
    step = 2.0 * math.pi / length
    hi_ang = ((freq * (split * jnp.arange(hi_count, dtype=jnp.int32)[None, :])) % length).astype(
        jnp.float32
    ) * step
    lo_ang = ((freq * jnp.arange(split, dtype=jnp.int32)[None, :]) % length).astype(
        jnp.float32
    ) * step
    hi_c, hi_s = jnp.cos(hi_ang)[:, :, None], jnp.sin(hi_ang)[:, :, None]
    lo_c, lo_s = jnp.cos(lo_ang)[:, None, :], jnp.sin(lo_ang)[:, None, :]
    cos_t = (hi_c * lo_c - hi_s * lo_s).reshape(length, length).astype(jnp.bfloat16)
    sin_t = (hi_c * lo_s + hi_s * lo_c).reshape(length, length).astype(jnp.bfloat16)
    return lax.optimization_barrier((cos_t, sin_t))


def phase_tables(bperp, tdays):
    grid_points = jnp.arange(HGRID * VGRID, dtype=jnp.int32)
    height_step = grid_points // VGRID
    speed_step = grid_points % VGRID
    quanta = (
        bperp[:, None] * height_step[None, :] + tdays[:, None] * speed_step[None, :]
    ) % PHASE_Q
    angles = quanta.astype(jnp.float32) * (2.0 * math.pi / PHASE_Q)
    phase_re = jnp.cos(angles).astype(jnp.bfloat16)
    phase_im = jnp.sin(angles).astype(jnp.bfloat16)
    upper = jnp.concatenate([phase_re, -phase_im], axis=1)
    lower = jnp.concatenate([phase_im, phase_re], axis=1)
    return jnp.concatenate([upper, lower], axis=0)


def shards(slc_re, slc_im, ref_date, gain, bperp, tdays, mask):
    date_dev, lines, rg_dev = slc_re.shape
    assert date_dev == 1
    n_date = lax.axis_size("date")
    n_rng = lax.axis_size("rng")
    cols = rg_dev // n_date
    lines_dev = lines // n_date
    pixel_total = lines * rg_dev * n_rng
    me = lax.axis_index("date")
    f32 = jnp.float32

    own_re = slc_re[0]
    own_im = slc_im[0]
    wide_re = own_re.astype(f32)
    wide_im = own_im.astype(f32)
    local = jnp.sum(wide_re * wide_re + wide_im * wide_im)
    own_sum = local
    for k in range(1, n_rng):
        own_sum = own_sum + lax.ppermute(
            local, "rng", [(r, (r + k) % n_rng) for r in range(n_rng)]
        )
    lane = jnp.arange(128)
    word = jnp.where(lane < 3, own_sum, 0.0)
    hi = lax.reduce_precision(word, exponent_bits=8, mantissa_bits=7)
    mid = lax.reduce_precision(word - hi, exponent_bits=8, mantissa_bits=7)
    lo = lax.reduce_precision(word - hi - mid, exponent_bits=8, mantissa_bits=7)
    word = jnp.where(lane == 0, hi, jnp.where(lane == 1, mid, lo))
    word = jnp.broadcast_to(word.astype(jnp.bfloat16), (n_date, 2 * cols, 128))

    both = jnp.stack([own_re.T, own_im.T]).reshape(2, cols, n_date, lines)
    both = both.transpose(2, 0, 1, 3).reshape(n_date, 2 * cols, lines)
    both = jnp.concatenate([both, word], axis=2)
    got = lax.all_to_all(both, "date", split_axis=0, concat_axis=0, tiled=True)
    sums = got[:, 0, lines:lines + 3].astype(f32)
    date_sums = (sums[:, 0] + sums[:, 1]) + sums[:, 2]
    scales = lax.rsqrt(date_sums / pixel_total + 1e-06)
    got = got[:, :, :lines].reshape(n_date, 2, cols, lines)
    x_re = got[:, 0].reshape(n_date * cols, lines)
    x_im = got[:, 1].reshape(n_date * cols, lines)

    ref_index = ref_date[0]
    ref_scale = scales[ref_index]
    rows = n_date * cols
    row_id = jnp.arange(rows, dtype=jnp.int32)[:, None]
    col_id = jnp.arange(rows, dtype=jnp.int32)[None, :]
    pick = (col_id == ref_index * cols + row_id % cols).astype(jnp.bfloat16)
    ref_re = jnp.dot(pick, x_re, preferred_element_type=f32) * ref_scale
    ref_im = jnp.dot(pick, x_im, preferred_element_type=f32) * ref_scale
    row_scale = jnp.repeat(scales, cols)[:, None]
    a_re = x_re.astype(f32) * row_scale
    a_im = x_im.astype(f32) * row_scale
    ifg_re = (a_re * ref_re + a_im * ref_im).astype(jnp.bfloat16)
    ifg_im = (a_im * ref_re - a_re * ref_im).astype(jnp.bfloat16)

    cos_t, sin_t = dft_table(lines)
    rows = n_date * cols
    stacked = jnp.concatenate([ifg_re, ifg_im], axis=0)
    fc = jnp.dot(stacked, cos_t, preferred_element_type=f32)
    fs = jnp.dot(stacked, sin_t, preferred_element_type=f32)
    spec_re = fc[:rows] + fs[rows:]
    spec_im = fc[rows:] - fs[:rows]
    weights = gain[None, :]
    held = jnp.concatenate(
        [(spec_re * weights).astype(jnp.bfloat16), (spec_im * weights).astype(jnp.bfloat16)],
        axis=0,
    )
    held = held.reshape(2, n_date, cols, lines).transpose(0, 2, 1, 3).reshape(2 * rows, lines)
    contract = (((0,), (1,)), ((), ()))
    bc = lax.dot_general(cos_t, held, contract, preferred_element_type=f32)
    bs = lax.dot_general(sin_t, held, contract, preferred_element_type=f32)
    filt_re = ((bc[:, :rows] - bs[:, rows:]) * (1.0 / lines)).astype(jnp.bfloat16)
    filt_im = ((bs[:, :rows] + bc[:, rows:]) * (1.0 / lines)).astype(jnp.bfloat16)
    blocks = []
    for c2 in range(cols):
        blocks.append(filt_re[:, c2 * n_date:(c2 + 1) * n_date])
        blocks.append(filt_im[:, c2 * n_date:(c2 + 1) * n_date])
    pair = jnp.concatenate(blocks, axis=1)
    got = lax.all_to_all(pair, "date", split_axis=0, concat_axis=0, tiled=True)
    z = got.reshape(n_date, lines_dev, cols, 2 * n_date).transpose(1, 2, 0, 3)
    z = z.reshape(lines_dev * cols * n_date, 2 * n_date)

    grid_size = HGRID * VGRID
    phase = phase_tables(bperp, tdays)
    spectra = jnp.dot(z, phase, preferred_element_type=f32)
    peri_re = spectra[:, :grid_size]
    peri_im = spectra[:, grid_size:]
    wide = z.astype(f32)
    pixel_power = jnp.sum(wide * wide, axis=1) / n_date
    mask_rows = lax.dynamic_slice_in_dim(mask, me * lines_dev, lines_dev, 0)
    mask_px = mask_rows.reshape(-1).astype(f32)
    result = (peri_re * peri_re + peri_im * peri_im) / (
        n_date * jnp.maximum(pixel_power, 1.0)
    )[:, None]
    result = result * mask_px[:, None]
    return result.reshape(lines_dev, cols * n_date, grid_size)


def solution(mesh):
    in_specs = (P("date", None, "rng"), P("date", None, "rng"), P(), P(), P(), P(), P(None, "rng"))
    out_specs = P("date", "rng", None)
    return jax.shard_map(shards, mesh=mesh, in_specs=in_specs, out_specs=out_specs, check_vma=False)
```

```python
import math

import jax
import jax.numpy as jnp
from jax import lax
from jax.sharding import PartitionSpec as P

HGRID = 16
VGRID = 16
PHASE_Q = 1024


def dft_table(length):
    split = 64
    hi_count = length // split
    freq = jnp.arange(length, dtype=jnp.int32)[:, None]
    step = 2.0 * math.pi / length
    hi_ang = ((freq * (split * jnp.arange(hi_count, dtype=jnp.int32)[None, :])) % length).astype(
        jnp.float32
    ) * step
    lo_ang = ((freq * jnp.arange(split, dtype=jnp.int32)[None, :]) % length).astype(
        jnp.float32
    ) * step
    hi_c, hi_s = jnp.cos(hi_ang)[:, :, None], jnp.sin(hi_ang)[:, :, None]
    lo_c, lo_s = jnp.cos(lo_ang)[:, None, :], jnp.sin(lo_ang)[:, None, :]
    cos_t = (hi_c * lo_c - hi_s * lo_s).reshape(length, length).astype(jnp.bfloat16)
    sin_t = (hi_c * lo_s + hi_s * lo_c).reshape(length, length).astype(jnp.bfloat16)
    return lax.optimization_barrier((cos_t, sin_t))


def phase_tables(bperp, tdays):
    grid_points = jnp.arange(HGRID * VGRID, dtype=jnp.int32)
    height_step = grid_points // VGRID
    speed_step = grid_points % VGRID
    quanta = (
        bperp[:, None] * height_step[None, :] + tdays[:, None] * speed_step[None, :]
    ) % PHASE_Q
    angles = quanta.astype(jnp.float32) * (2.0 * math.pi / PHASE_Q)
    phase_re = jnp.cos(angles).astype(jnp.bfloat16)
    phase_im = jnp.sin(angles).astype(jnp.bfloat16)
    upper = jnp.concatenate([phase_re, -phase_im], axis=1)
    lower = jnp.concatenate([phase_im, phase_re], axis=1)
    return jnp.concatenate([upper, lower], axis=0)


def shards(slc_re, slc_im, ref_date, gain, bperp, tdays, mask):
    date_dev, lines, rg_dev = slc_re.shape
    assert date_dev == 1
    n_date = lax.axis_size("date")
    n_rng = lax.axis_size("rng")
    cols = rg_dev // n_date
    lines_dev = lines // n_date
    pixel_total = lines * rg_dev * n_rng
    me = lax.axis_index("date")
    f32 = jnp.float32

    own_re = slc_re[0]
    own_im = slc_im[0]
    wide_re = own_re.astype(f32)
    wide_im = own_im.astype(f32)
    local = jnp.sum(wide_re * wide_re + wide_im * wide_im)
    own_sum = local
    for k in range(1, n_rng):
        own_sum = own_sum + lax.ppermute(
            local, "rng", [(r, (r + k) % n_rng) for r in range(n_rng)]
        )
    lane = jnp.arange(128)
    word = jnp.where(lane < 3, own_sum, 0.0)
    hi = lax.reduce_precision(word, exponent_bits=8, mantissa_bits=7)
    mid = lax.reduce_precision(word - hi, exponent_bits=8, mantissa_bits=7)
    lo = lax.reduce_precision(word - hi - mid, exponent_bits=8, mantissa_bits=7)
    word = jnp.where(lane == 0, hi, jnp.where(lane == 1, mid, lo))
    word = jnp.broadcast_to(word.astype(jnp.bfloat16), (n_date, 2 * cols, 128))

    both = jnp.stack([own_re.T, own_im.T]).reshape(2, cols, n_date, lines)
    both = both.transpose(2, 0, 1, 3).reshape(n_date, 2 * cols, lines)
    both = jnp.concatenate([both, word], axis=2)
    got = lax.all_to_all(both, "date", split_axis=0, concat_axis=0, tiled=True)
    sums = got[:, 0, lines:lines + 3].astype(f32)
    date_sums = (sums[:, 0] + sums[:, 1]) + sums[:, 2]
    scales = lax.rsqrt(date_sums / pixel_total + 1e-06)
    got = got[:, :, :lines].reshape(n_date, 2, cols, lines)
    x_re = got[:, 0].reshape(n_date * cols, lines)
    x_im = got[:, 1].reshape(n_date * cols, lines)

    ref_index = ref_date[0]
    ref_scale = scales[ref_index]
    rows = n_date * cols
    row_id = jnp.arange(rows, dtype=jnp.int32)[:, None]
    col_id = jnp.arange(rows, dtype=jnp.int32)[None, :]
    pick = (col_id == ref_index * cols + row_id % cols).astype(jnp.bfloat16)
    ref_re = jnp.dot(pick, x_re, preferred_element_type=f32) * ref_scale
    ref_im = jnp.dot(pick, x_im, preferred_element_type=f32) * ref_scale
    row_scale = jnp.repeat(scales, cols)[:, None]
    a_re = x_re.astype(f32) * row_scale
    a_im = x_im.astype(f32) * row_scale
    ifg_re = (a_re * ref_re + a_im * ref_im).astype(jnp.bfloat16)
    ifg_im = (a_im * ref_re - a_re * ref_im).astype(jnp.bfloat16)

    cos_t, sin_t = dft_table(lines)
    rows = n_date * cols
    stacked = jnp.concatenate([ifg_re, ifg_im], axis=0)
    fs = jnp.dot(stacked, sin_t, preferred_element_type=f32)
    stacked_after, fs = lax.optimization_barrier((stacked, fs))
    fc = jnp.dot(stacked_after, cos_t, preferred_element_type=f32)
    spec_re = fc[:rows] + fs[rows:]
    spec_im = fc[rows:] - fs[:rows]
    weights = gain[None, :]
    held = jnp.concatenate(
        [(spec_re * weights).astype(jnp.bfloat16), (spec_im * weights).astype(jnp.bfloat16)],
        axis=0,
    )
    bc = jnp.dot(held, cos_t, preferred_element_type=f32)
    bs = jnp.dot(held, sin_t, preferred_element_type=f32)
    filt_re = ((bc[:rows] - bs[rows:]) * (1.0 / lines)).astype(jnp.bfloat16)
    filt_im = ((bs[:rows] + bc[rows:]) * (1.0 / lines)).astype(jnp.bfloat16)

    pair = jnp.concatenate([filt_re, filt_im], axis=0).reshape(2, n_date, cols, lines)
    pair = pair.transpose(2, 0, 1, 3).reshape(2 * rows, lines).T
    got = lax.all_to_all(pair, "date", split_axis=0, concat_axis=0, tiled=True)
    z = got.reshape(n_date, lines_dev, cols, 2 * n_date).transpose(1, 2, 0, 3)
    z = z.reshape(lines_dev * cols * n_date, 2 * n_date)

    grid_size = HGRID * VGRID
    phase = phase_tables(bperp, tdays)
    spectra = jnp.dot(z, phase, preferred_element_type=f32)
    peri_re = spectra[:, :grid_size]
    peri_im = spectra[:, grid_size:]
    wide = z.astype(f32)
    pixel_power = jnp.sum(wide * wide, axis=1) / n_date
    mask_rows = lax.dynamic_slice_in_dim(mask, me * lines_dev, lines_dev, 0)
    mask_px = mask_rows.reshape(-1).astype(f32)
    result = (peri_re * peri_re + peri_im * peri_im) / (
        n_date * jnp.maximum(pixel_power, 1.0)
    )[:, None]
    result = result * mask_px[:, None]
    return result.reshape(lines_dev, cols * n_date, grid_size)


def solution(mesh):
    in_specs = (P("date", None, "rng"), P("date", None, "rng"), P(), P(), P(), P(), P(None, "rng"))
    out_specs = P("date", "rng", None)
    return jax.shard_map(shards, mesh=mesh, in_specs=in_specs, out_specs=out_specs, check_vma=False)
```
